32 devices in a mesh: groups: 2 (over y), tok: 8 (over z, x), section: 2 (over core).
Axes of the slice: x: 2, y: 2, z: 4, core: 2. Of those that a mesh axis runs over, the one named last changes fastest.
Arguments:
- inputs: bfloat16 [4, 1024, 2048], P('groups', 'tok'), parts along dimension 0, may hold values from -11 to 11
- obs: bfloat16 [2048, 2048], P(('groups', 'tok')), parts along dimension 0, may hold values from -11 to 11
- weights: bfloat16 [2, 2048, 2048], P('section', 'tok'), may hold values from -0.125 to 0.125
- gains: float32 [2, 2048], P('section'), may hold values from 0.25 to 1.75
Outputs:
- section_grads: bfloat16 [2, 4, 1024, 2048], P('section', 'groups', 'tok'), parts along dimension 1
- energy: float32 [2], P('groups'), parts along dimension 0
The draws below stay inside these ranges and needn't reach their ends.
There are 2 independent parts, one for each index of `groups`. The reference program is written for one: setup_inputs(seed, part) draws one part's arguments, and reference() takes and returns one part's arrays. A program takes and returns all parts, laid end to end along the dimension named above; an argument that names none is the same for every part. Nothing has to cross between parts.
All inputs are finite; a program needn't handle non-finite values.
Results may differ from the reference program's by a relative error of at most 0.008.
Values may be sent and summed in bfloat16 or wider, within the bound.
No kernel may reach another device: no remote copies, remote signals or barrier semaphores. Data moves between devices by JAX's collectives and lax.ppermute only.
A program may use at most 64 MiB of HBM per device.

```python
import math
import jax
import jax.numpy as jnp
from jax import lax

D = 2048
MEMBERS = 2
TOKENS = 1024


def rising_field(key, rows, shape):
    normal_key, row_key = jax.random.split(key)
    position = jnp.arange(rows, dtype=jnp.float32) / rows
    normal_part = jnp.clip(jax.random.normal(normal_key, shape, jnp.float32), -4.0, 4.0)
    row_rise = 0.6 * jnp.exp(position * math.log(3.0))
    row_shape = shape[:-1] + (1,)
    row_factor = jnp.exp(jax.random.uniform(row_key, row_shape, jnp.float32, -0.35, 0.35))
    return normal_part * row_rise[:, None] * row_factor


def draw_inputs(key, part):
    field = rising_field(jax.random.fold_in(key, 11), TOKENS, (MEMBERS, TOKENS, D))
    return field.astype(jnp.bfloat16)


def draw_obs(key, part):
    field = rising_field(jax.random.fold_in(key, 23), TOKENS, (TOKENS, D))
    return field.astype(jnp.bfloat16)


def levels(stream_key, dims, pieces, low, high):
    def one(dim, parts):
        steps = jax.random.uniform(jax.random.fold_in(jax.random.fold_in(stream_key, 6), dim), (parts,), jnp.float32, low / len(pieces), high / len(pieces))
        return jnp.repeat(jnp.exp(steps), dims[dim] // parts).reshape((-1,) + (1,) * (len(dims) - dim - 1))

    factor_of = one(*pieces[0])
    for cut in pieces[1:]:
        factor_of = factor_of * one(*cut)
    return factor_of


def bell_draw(rng, dims, width, most, cuts=(), kind=jnp.bfloat16):
    level = levels(rng, dims, cuts, -0.22, 0.18) if cuts else 1.0
    values = jax.random.normal(rng, dims, jnp.float32) * width * level
    return jnp.minimum(jnp.maximum(values, -most), most).astype(kind)


def setup_inputs(seed: int = 0, part: int = 0) -> dict:
    arg_keys = jax.random.split(jax.random.key(seed), 5)
    part_keys = jax.random.split(jax.random.fold_in(arg_keys[4], part), 5)
    return {
        "inputs": draw_inputs(jax.random.fold_in(jax.random.fold_in(arg_keys[4], part), 71), part),
        "obs": draw_obs(jax.random.fold_in(jax.random.fold_in(arg_keys[4], part), 71), part),
        "weights": bell_draw(arg_keys[2], (2, D, D), D ** -0.5, 0.125, ((0, 2), (1, 8))),
        "gains": jnp.clip(1.0 + 0.15 * jax.random.normal(arg_keys[3], (2, D), jnp.float32), 0.25, 1.75),
    }


epsilon = 1e-05
gelu_scale = math.sqrt(2.0 / math.pi)
cubic_term = 0.044715

def gelu_value(pre_act):
    inner = jnp.tanh(gelu_scale * (pre_act + cubic_term * pre_act * pre_act * pre_act))
    return 0.5 * pre_act * (1.0 + inner)

def gelu_slope(pre_act):
    inner = jnp.tanh(gelu_scale * (pre_act + cubic_term * pre_act * pre_act * pre_act))
    return 0.5 * (1.0 + inner) + 0.5 * pre_act * (1.0 - inner * inner) * gelu_scale * (1.0 + 3.0 * cubic_term * pre_act * pre_act)

def section_forward(rows_in, gain, weight):
    values = rows_in.astype(jnp.float32)
    row_mean = lax.optimization_barrier(jnp.mean(values, axis=-1, keepdims=True))
    centred = values - row_mean
    inv_std = lax.rsqrt(lax.optimization_barrier(jnp.mean(centred * centred, axis=-1, keepdims=True)) + epsilon)
    unit_rows = centred * inv_std
    normed = (unit_rows * gain).astype(jnp.bfloat16)
    pre_act = jnp.dot(normed, weight, preferred_element_type=jnp.float32)
    output = (values + gelu_value(pre_act)).astype(jnp.bfloat16)
    return (output, unit_rows, inv_std, pre_act)

def section_backward(grad_out, gain, weight, unit_rows, inv_std, pre_act):
    grad_f = grad_out.astype(jnp.float32)
    grad_pre = (grad_f * gelu_slope(pre_act)).astype(jnp.bfloat16)
    grad_norm = jnp.dot(grad_pre, weight.T, preferred_element_type=jnp.float32)
    scaled = grad_norm * gain
    grad_in = grad_f + inv_std * (scaled - lax.optimization_barrier(jnp.mean(scaled, axis=-1, keepdims=True)) - unit_rows * lax.optimization_barrier(jnp.mean(scaled * unit_rows, axis=-1, keepdims=True)))
    return grad_in.astype(jnp.bfloat16)

def score_terms(member_gram, member_obs, obs_sq, size):
    count = member_gram.shape[0]
    diag_vals = jnp.diagonal(member_gram)
    apart = diag_vals[:, None] + diag_vals[None, :] - 2.0 * member_gram
    same = jnp.eye(count, dtype=jnp.float32)
    others = 1.0 - same
    pair_dist = jnp.sqrt(jnp.where(same > 0.5, size, apart) / size + epsilon)
    to_obs = jnp.sqrt((diag_vals - 2.0 * member_obs + obs_sq) / size + epsilon)
    energy = jnp.mean(to_obs) - jnp.sum(others * pair_dist) / (2.0 * count * (count - 1))
    pair_coeff = others / (count * (count - 1) * pair_dist)
    obs_coeff = 1.0 / (count * to_obs)
    member_coeff = pair_coeff + same * (obs_coeff - lax.optimization_barrier(jnp.sum(pair_coeff, axis=1)))[:, None]
    return (energy, member_coeff, -obs_coeff)

def reference(inputs, obs, weights, gains):
    members = inputs.shape[0]
    firsts = []
    seconds = []
    for member in range(members):
        first = section_forward(inputs[member], gains[0], weights[0])
        second = section_forward(first[0], gains[1], weights[1])
        firsts.append(first)
        seconds.append(second)
    stacked = jnp.stack([item[0] for item in seconds]).astype(jnp.float32)
    obs_f = obs.astype(jnp.float32)
    member_gram = jnp.einsum('mtd,ntd->mn', stacked, stacked)
    member_obs = jnp.einsum('mtd,td->m', stacked, obs_f)
    obs_sq = jnp.sum(obs_f * obs_f)
    size = float(obs.shape[0] * obs.shape[1])
    energy, member_coeff, obs_coeff = score_terms(member_gram, member_obs, obs_sq, size)
    first_grads = []
    second_grads = []
    for member in range(members):
        cotangent = jnp.einsum('k,ktd->td', member_coeff[member], stacked) + obs_coeff[member] * obs_f
        second = seconds[member]
        grad_mid = section_backward(cotangent, gains[1], weights[1], second[1], second[2], second[3])
        first = firsts[member]
        grad_first = section_backward(grad_mid.astype(jnp.float32), gains[0], weights[0], first[1], first[2], first[3])
        first_grads.append(grad_first)
        second_grads.append(grad_mid)
    section_grads = jnp.stack([jnp.stack(first_grads), jnp.stack(second_grads)])
    return (section_grads, jnp.reshape(energy, (1,)).astype(jnp.float32))
```

```python
import math

import jax
import jax.numpy as jnp
from jax import lax
from jax.sharding import PartitionSpec as P

epsilon = 1e-05
gelu_scale = math.sqrt(2.0 / math.pi)
cubic_term = 0.044715

RING_GATHER = True


def shifted(x, axis, by):
    size = lax.axis_size(axis)
    pairs = [(i, i + by) for i in range(size) if 0 <= i + by < size]
    return lax.ppermute(x, axis, pairs)


def gelu_value(pre_act):
    inner = jnp.tanh(gelu_scale * (pre_act + cubic_term * pre_act * pre_act * pre_act))
    return 0.5 * pre_act * (1.0 + inner)


def gelu_slope(pre_act):
    inner = jnp.tanh(gelu_scale * (pre_act + cubic_term * pre_act * pre_act * pre_act))
    return 0.5 * (1.0 + inner) + 0.5 * pre_act * (1.0 - inner * inner) * gelu_scale * (
        1.0 + 3.0 * cubic_term * pre_act * pre_act
    )


def section_forward(rows_in, gain, weight):
    values = rows_in.astype(jnp.float32)
    row_mean = jnp.mean(values, axis=-1, keepdims=True)
    centred = values - row_mean
    inv_std = lax.rsqrt(jnp.mean(centred * centred, axis=-1, keepdims=True) + epsilon)
    unit_rows = centred * inv_std
    normed = (unit_rows * gain).astype(jnp.bfloat16)
    pre_act = jnp.dot(normed, weight, preferred_element_type=jnp.float32)
    output = (values + gelu_value(pre_act)).astype(jnp.bfloat16)
    return (output, unit_rows, inv_std, pre_act)


def section_backward(grad_out, gain, weight, unit_rows, inv_std, pre_act):
    grad_pre = (grad_out * gelu_slope(pre_act)).astype(jnp.bfloat16)
    grad_norm = lax.dot_general(
        grad_pre, weight, (((1,), (1,)), ((), ())), preferred_element_type=jnp.float32
    )
    scaled = grad_norm * gain
    grad_in = grad_out + inv_std * (
        scaled
        - jnp.mean(scaled, axis=-1, keepdims=True)
        - unit_rows * jnp.mean(scaled * unit_rows, axis=-1, keepdims=True)
    )
    return grad_in.astype(jnp.bfloat16)


def score_terms(member_gram, member_obs, obs_sq, size):
    count = member_gram.shape[0]
    diag_vals = jnp.diagonal(member_gram)
    apart = diag_vals[:, None] + diag_vals[None, :] - 2.0 * member_gram
    same = jnp.eye(count, dtype=jnp.float32)
    others = 1.0 - same
    pair_dist = jnp.sqrt(jnp.where(same > 0.5, size, apart) / size + epsilon)
    to_obs = jnp.sqrt((diag_vals - 2.0 * member_obs + obs_sq) / size + epsilon)
    energy = jnp.mean(to_obs) - jnp.sum(others * pair_dist) / (2.0 * count * (count - 1))
    pair_coeff = others / (count * (count - 1) * pair_dist)
    obs_coeff = 1.0 / (count * to_obs)
    member_coeff = pair_coeff + same * (obs_coeff - jnp.sum(pair_coeff, axis=1))[:, None]
    return (energy, member_coeff, -obs_coeff)


def snake_ring(n):
    if n % 2:
        return list(range(n))
    return list(range(0, n, 2)) + list(range(n - 1, 0, -2))


def ring_gather(local, axis):
    n = lax.axis_size(axis)
    rows, cols = local.shape
    if n == 1:
        return local
    ring = snake_ring(n)
    pos_of = [0] * n
    for p, t in enumerate(ring):
        pos_of[t] = p
    me = lax.axis_index(axis)
    my_pos = jnp.asarray(pos_of, jnp.int32)[me]
    ring_arr = jnp.asarray(ring, jnp.int32)
    cw = [(ring[i], ring[(i + 1) % n]) for i in range(n)]
    ccw = [(ring[(i + 1) % n], ring[i]) for i in range(n)]
    half = cols // 2
    left = local[:, :half]
    right = local[:, half:]
    full = jnp.zeros((n * rows, cols), local.dtype)
    full = lax.dynamic_update_slice(full, local, (me * rows, 0))
    for k in range(1, n):
        left = lax.ppermute(left, axis, cw)
        right = lax.ppermute(right, axis, ccw)
        from_left = ring_arr[(my_pos - k) % n]
        from_right = ring_arr[(my_pos + k) % n]
        full = lax.dynamic_update_slice(full, left, (from_left * rows, 0))
        full = lax.dynamic_update_slice(full, right, (from_right * rows, half))
    return full


def tree_sum(v, axis):
    n = lax.axis_size(axis)
    if n & (n - 1):
        return lax.psum(v, axis)
    b = 1
    while b < n:
        v = v + lax.ppermute(v, axis, [(i, i ^ b) for i in range(n)])
        b *= 2
    return v


def per_device(inputs, obs, weights, gains):
    sec = lax.axis_index("section")
    on_first = sec == 0
    gain = gains[0]
    tok_rows = obs.shape[0]
    width = obs.shape[1]
    size = float(tok_rows * lax.axis_size("tok") * width)

    obs_sq = jnp.einsum("rd,rd->", obs, obs, preferred_element_type=jnp.float32)

    if RING_GATHER:
        weight = ring_gather(weights[0], "tok")
    else:
        weight = lax.all_gather(weights, "tok", axis=1, tiled=True)[0]

    fa = section_forward(inputs[0], gain, weight)
    arrived0 = shifted(fa[0], "section", 1)
    fb = section_forward(jnp.where(on_first, inputs[1], arrived0), gain, weight)
    arrived1 = shifted(fb[0], "section", 1)
    fc = section_forward(arrived1, gain, weight)

    y0 = fb[0]
    y1 = fc[0]
    gram = jnp.einsum(
        "mrd,nrd->mn", jnp.stack([y0, y1]), jnp.stack([y0, y1]),
        preferred_element_type=jnp.float32,
    )
    obs_part = jnp.einsum(
        "mrd,rd->m", jnp.stack([y0, y1]), obs, preferred_element_type=jnp.float32
    )
    packed = jnp.concatenate([gram.reshape(4), obs_part, obs_sq.reshape(1)])
    packed = tree_sum(packed, "tok")
    member_gram = packed[:4].reshape(2, 2)
    obs_rows = packed[4:6]
    obs_total = packed[6]
    energy, member_coeff, obs_coeff = score_terms(member_gram, obs_rows, obs_total, size)
    energy_arr = jnp.reshape(energy, (1,))
    energy_peer = shifted(energy_arr, "section", -1)
    energy_out = jnp.where(on_first, energy_peer, energy_arr)

    obs_f = obs.astype(jnp.float32)
    y0f = y0.astype(jnp.float32)
    y1f = y1.astype(jnp.float32)

    def cotangent(m):
        return member_coeff[m, 0] * y0f + member_coeff[m, 1] * y1f + obs_coeff[m] * obs_f

    d0 = section_backward(cotangent(0), gain, weight, fb[1], fb[2], fb[3])
    back0 = shifted(d0, "section", -1)
    g1 = jnp.where(on_first, back0.astype(jnp.float32), cotangent(1))
    h1 = jnp.where(on_first, fa[1], fc[1])
    q1 = jnp.where(on_first, fa[2], fc[2])
    p1 = jnp.where(on_first, fa[3], fc[3])
    d1 = section_backward(g1, gain, weight, h1, q1, p1)
    back1 = shifted(d1, "section", -1)
    d2 = section_backward(back1.astype(jnp.float32), gain, weight, fb[1], fb[2], fb[3])

    first_m0 = jnp.where(on_first, d1, d0)
    first_m1 = jnp.where(on_first, d2, d1)
    grads = jnp.stack([first_m0, first_m1])
    return (grads[None], energy_out)


def solution(mesh):
    in_specs = (
        P("groups", "tok", None),
        P(("groups", "tok"), None),
        P("section", "tok", None),
        P("section", None),
    )
    out_specs = (P("section", "groups", "tok", None), P("groups"))
    return jax.shard_map(
        per_device, mesh=mesh, in_specs=in_specs, out_specs=out_specs, check_vma=False
    )
```

```python
import math

import jax
import jax.numpy as jnp
from jax import lax
from jax.sharding import PartitionSpec as P

epsilon = 1e-05
gelu_scale = math.sqrt(2.0 / math.pi)
cubic_term = 0.044715

RING_GATHER = True


def shifted(x, axis, by):
    size = lax.axis_size(axis)
    pairs = [(i, i + by) for i in range(size) if 0 <= i + by < size]
    return lax.ppermute(x, axis, pairs)


def gelu_value(pre_act):
    inner = jnp.tanh(gelu_scale * (pre_act + cubic_term * pre_act * pre_act * pre_act))
    return 0.5 * pre_act * (1.0 + inner)


def gelu_slope(pre_act):
    inner = jnp.tanh(gelu_scale * (pre_act + cubic_term * pre_act * pre_act * pre_act))
    return 0.5 * (1.0 + inner) + 0.5 * pre_act * (1.0 - inner * inner) * gelu_scale * (
        1.0 + 3.0 * cubic_term * pre_act * pre_act
    )


def section_forward(rows_in, gain, weight):
    values = rows_in.astype(jnp.float32)
    row_mean = jnp.mean(values, axis=-1, keepdims=True)
    centred = values - row_mean
    inv_std = lax.rsqrt(jnp.mean(centred * centred, axis=-1, keepdims=True) + epsilon)
    unit_rows = centred * inv_std
    normed = (unit_rows * gain).astype(jnp.bfloat16)
    pre_act = jnp.dot(normed, weight, preferred_element_type=jnp.float32)
    output = (values + gelu_value(pre_act)).astype(jnp.bfloat16)
    return (output, unit_rows, inv_std, pre_act)


def section_backward(grad_out, gain, weight, unit_rows, inv_std, pre_act):
    grad_pre = (grad_out * gelu_slope(pre_act)).astype(jnp.bfloat16)
    grad_norm = lax.dot_general(
        grad_pre, weight, (((1,), (1,)), ((), ())), preferred_element_type=jnp.float32
    )
    scaled = grad_norm * gain
    grad_in = grad_out + inv_std * (
        scaled
        - jnp.mean(scaled, axis=-1, keepdims=True)
        - unit_rows * jnp.mean(scaled * unit_rows, axis=-1, keepdims=True)
    )
    return grad_in.astype(jnp.bfloat16)


def score_terms(member_gram, member_obs, obs_sq, size):
    count = member_gram.shape[0]
    diag_vals = jnp.diagonal(member_gram)
    apart = diag_vals[:, None] + diag_vals[None, :] - 2.0 * member_gram
    same = jnp.eye(count, dtype=jnp.float32)
    others = 1.0 - same
    pair_dist = jnp.sqrt(jnp.where(same > 0.5, size, apart) / size + epsilon)
    to_obs = jnp.sqrt((diag_vals - 2.0 * member_obs + obs_sq) / size + epsilon)
    energy = jnp.mean(to_obs) - jnp.sum(others * pair_dist) / (2.0 * count * (count - 1))
    pair_coeff = others / (count * (count - 1) * pair_dist)
    obs_coeff = 1.0 / (count * to_obs)
    member_coeff = pair_coeff + same * (obs_coeff - jnp.sum(pair_coeff, axis=1))[:, None]
    return (energy, member_coeff, -obs_coeff)


def snake_ring(n):
    if n % 2:
        return list(range(n))
    return list(range(0, n, 2)) + list(range(n - 1, 0, -2))


def ring_gather(local, axis):
    n = lax.axis_size(axis)
    rows, cols = local.shape
    if n == 1:
        return local
    ring = snake_ring(n)
    pos_of = [0] * n
    for p, t in enumerate(ring):
        pos_of[t] = p
    me = lax.axis_index(axis)
    my_pos = jnp.asarray(pos_of, jnp.int32)[me]
    ring_arr = jnp.asarray(ring, jnp.int32)
    cw = [(ring[i], ring[(i + 1) % n]) for i in range(n)]
    ccw = [(ring[(i + 1) % n], ring[i]) for i in range(n)]
    half = cols // 2
    left = local[:, :half]
    right = local[:, half:]
    full = jnp.zeros((n * rows, cols), local.dtype)
    full = lax.dynamic_update_slice(full, local, (me * rows, 0))
    for k in range(1, n):
        left = lax.ppermute(left, axis, cw)
        right = lax.ppermute(right, axis, ccw)
        from_left = ring_arr[(my_pos - k) % n]
        from_right = ring_arr[(my_pos + k) % n]
        full = lax.dynamic_update_slice(full, left, (from_left * rows, 0))
        full = lax.dynamic_update_slice(full, right, (from_right * rows, half))
    return full


def tree_sum(v, axis):
    n = lax.axis_size(axis)
    if n & (n - 1):
        return lax.psum(v, axis)
    b = 1
    while b < n:
        v = v + lax.ppermute(v, axis, [(i, i ^ b) for i in range(n)])
        b *= 2
    return v


def per_device(inputs, obs, weights, gains):
    sec = lax.axis_index("section")
    on_first = sec == 0
    gain = gains[0]
    tok_rows = obs.shape[0]
    width = obs.shape[1]
    size = float(tok_rows * lax.axis_size("tok") * width)

    obs_sq = jnp.einsum("rd,rd->", obs, obs, preferred_element_type=jnp.float32)

    if RING_GATHER:
        weight = ring_gather(weights[0], "tok")
    else:
        weight = lax.all_gather(weights, "tok", axis=1, tiled=True)[0]

    members = inputs.shape[0]
    rows_all = inputs.reshape(members * tok_rows, width)

    fa = section_forward(rows_all, gain, weight)
    arrived = shifted(fa[0], "section", 1)
    fb = section_forward(arrived, gain, weight)

    y = fb[0].astype(jnp.float32).reshape(members, tok_rows, width)
    obs_f = obs.astype(jnp.float32)
    terms = []
    for m in range(members):
        for k in range(members):
            terms.append(jnp.sum(y[m] * y[k]))
    for m in range(members):
        terms.append(jnp.sum(y[m] * obs_f))
    terms.append(obs_sq)
    packed = tree_sum(jnp.stack(terms), "tok")
    member_gram = packed[: members * members].reshape(members, members)
    obs_rows = packed[members * members : members * members + members]
    obs_total = packed[members * members + members]
    energy, member_coeff, obs_coeff = score_terms(member_gram, obs_rows, obs_total, size)
    energy_arr = jnp.reshape(energy, (1,))
    energy_peer = shifted(energy_arr, "section", -1)
    energy_out = jnp.where(on_first, energy_peer, energy_arr)

    cots = []
    for m in range(members):
        c = obs_coeff[m] * obs_f
        for k in range(members):
            c = c + member_coeff[m, k] * y[k]
        cots.append(c)
    cot = jnp.concatenate(cots, axis=0)

    da = section_backward(cot, gain, weight, fb[1], fb[2], fb[3])
    back = shifted(da, "section", -1)
    db = section_backward(back.astype(jnp.float32), gain, weight, fa[1], fa[2], fa[3])
    grads = jnp.where(on_first, db, da).reshape(members, tok_rows, width)
    return (grads[None], energy_out)


def solution(mesh):
    in_specs = (
        P("groups", "tok", None),
        P(("groups", "tok"), None),
        P("section", "tok", None),
        P("section", None),
    )
    out_specs = (P("section", "groups", "tok", None), P("groups"))
    return jax.shard_map(
        per_device, mesh=mesh, in_specs=in_specs, out_specs=out_specs, check_vma=False
    )
```

```python
import math

import jax
import jax.numpy as jnp
from jax import lax
from jax.sharding import PartitionSpec as P

epsilon = 1e-05
gelu_scale = math.sqrt(2.0 / math.pi)
cubic_term = 0.044715

RING_GATHER = True


def shifted(x, axis, by):
    size = lax.axis_size(axis)
    pairs = [(i, i + by) for i in range(size) if 0 <= i + by < size]
    return lax.ppermute(x, axis, pairs)


def gelu_value(pre_act):
    inner = jnp.tanh(gelu_scale * (pre_act + cubic_term * pre_act * pre_act * pre_act))
    return 0.5 * pre_act * (1.0 + inner)


def gelu_slope(pre_act):
    inner = jnp.tanh(gelu_scale * (pre_act + cubic_term * pre_act * pre_act * pre_act))
    return 0.5 * (1.0 + inner) + 0.5 * pre_act * (1.0 - inner * inner) * gelu_scale * (
        1.0 + 3.0 * cubic_term * pre_act * pre_act
    )


def section_forward(rows_in, gain, weight):
    values = rows_in.astype(jnp.float32)
    row_mean = jnp.mean(values, axis=-1, keepdims=True)
    centred = values - row_mean
    inv_std = lax.rsqrt(jnp.mean(centred * centred, axis=-1, keepdims=True) + epsilon)
    unit_rows = centred * inv_std
    normed = (unit_rows * gain).astype(jnp.bfloat16)
    pre_act = jnp.dot(normed, weight, preferred_element_type=jnp.float32)
    output = (values + gelu_value(pre_act)).astype(jnp.bfloat16)
    return (output, unit_rows, inv_std, pre_act)


def section_backward(grad_out, gain, weight, unit_rows, inv_std, pre_act):
    grad_pre = (grad_out * gelu_slope(pre_act)).astype(jnp.bfloat16)
    grad_norm = lax.dot_general(
        grad_pre, weight, (((1,), (1,)), ((), ())), preferred_element_type=jnp.float32
    )
    scaled = grad_norm * gain
    grad_in = grad_out + inv_std * (
        scaled
        - jnp.mean(scaled, axis=-1, keepdims=True)
        - unit_rows * jnp.mean(scaled * unit_rows, axis=-1, keepdims=True)
    )
    return grad_in.astype(jnp.bfloat16)


def score_terms(member_gram, member_obs, obs_sq, size):
    count = member_gram.shape[0]
    diag_vals = jnp.diagonal(member_gram)
    apart = diag_vals[:, None] + diag_vals[None, :] - 2.0 * member_gram
    same = jnp.eye(count, dtype=jnp.float32)
    others = 1.0 - same
    pair_dist = jnp.sqrt(jnp.where(same > 0.5, size, apart) / size + epsilon)
    to_obs = jnp.sqrt((diag_vals - 2.0 * member_obs + obs_sq) / size + epsilon)
    energy = jnp.mean(to_obs) - jnp.sum(others * pair_dist) / (2.0 * count * (count - 1))
    pair_coeff = others / (count * (count - 1) * pair_dist)
    obs_coeff = 1.0 / (count * to_obs)
    member_coeff = pair_coeff + same * (obs_coeff - jnp.sum(pair_coeff, axis=1))[:, None]
    return (energy, member_coeff, -obs_coeff)


def snake_ring(n):
    if n % 2:
        return list(range(n))
    return list(range(0, n, 2)) + list(range(n - 1, 0, -2))


def ring_gather(local, axis, pieces=2):
    n = lax.axis_size(axis)
    rows, cols = local.shape
    if n == 1:
        return local
    ring = snake_ring(n)
    pos_of = [0] * n
    for p, t in enumerate(ring):
        pos_of[t] = p
    me = lax.axis_index(axis)
    my_pos = jnp.asarray(pos_of, jnp.int32)[me]
    ring_arr = jnp.asarray(ring, jnp.int32)
    cw = [(ring[i], ring[(i + 1) % n]) for i in range(n)]
    ccw = [(ring[(i + 1) % n], ring[i]) for i in range(n)]
    width = cols // (2 * pieces)
    parts = [local[:, j * width:(j + 1) * width] for j in range(2 * pieces)]
    full = jnp.zeros((n * rows, cols), local.dtype)
    full = lax.dynamic_update_slice(full, local, (me * rows, 0))
    for k in range(1, n):
        from_cw = ring_arr[(my_pos - k) % n]
        from_ccw = ring_arr[(my_pos + k) % n]
        for j in range(2 * pieces):
            clockwise = j % 2 == 0
            parts[j] = lax.ppermute(parts[j], axis, cw if clockwise else ccw)
            origin = from_cw if clockwise else from_ccw
            full = lax.dynamic_update_slice(full, parts[j], (origin * rows, j * width))
    return full


def tree_sum(v, axis):
    n = lax.axis_size(axis)
    if n & (n - 1):
        return lax.psum(v, axis)
    b = 1
    while b < n:
        v = v + lax.ppermute(v, axis, [(i, i ^ b) for i in range(n)])
        b *= 2
    return v


def per_device(inputs, obs, weights, gains):
    sec = lax.axis_index("section")
    on_first = sec == 0
    gain = gains[0]
    tok_rows = obs.shape[0]
    width = obs.shape[1]
    size = float(tok_rows * lax.axis_size("tok") * width)

    obs_sq = jnp.einsum("rd,rd->", obs, obs, preferred_element_type=jnp.float32)

    if RING_GATHER:
        weight = ring_gather(weights[0], "tok")
    else:
        weight = lax.all_gather(weights, "tok", axis=1, tiled=True)[0]

    members = inputs.shape[0]
    rows_all = inputs.reshape(members * tok_rows, width)

    fa = section_forward(rows_all, gain, weight)
    arrived = shifted(fa[0], "section", 1)
    fb = section_forward(arrived, gain, weight)

    y = fb[0].astype(jnp.float32).reshape(members, tok_rows, width)
    obs_f = obs.astype(jnp.float32)
    terms = []
    for m in range(members):
        for k in range(members):
            terms.append(jnp.sum(y[m] * y[k]))
    for m in range(members):
        terms.append(jnp.sum(y[m] * obs_f))
    terms.append(obs_sq)
    packed = tree_sum(jnp.stack(terms), "tok")
    member_gram = packed[: members * members].reshape(members, members)
    obs_rows = packed[members * members : members * members + members]
    obs_total = packed[members * members + members]
    energy, member_coeff, obs_coeff = score_terms(member_gram, obs_rows, obs_total, size)
    energy_arr = jnp.reshape(energy, (1,))
    energy_peer = shifted(energy_arr, "section", -1)
    energy_out = jnp.where(on_first, energy_peer, energy_arr)

    cots = []
    for m in range(members):
        c = obs_coeff[m] * obs_f
        for k in range(members):
            c = c + member_coeff[m, k] * y[k]
        cots.append(c)
    cot = jnp.concatenate(cots, axis=0)

    da = section_backward(cot, gain, weight, fb[1], fb[2], fb[3])
    back = shifted(da, "section", -1)
    db = section_backward(back.astype(jnp.float32), gain, weight, fa[1], fa[2], fa[3])
    grads = jnp.where(on_first, db, da).reshape(members, tok_rows, width)
    return (grads[None], energy_out)


def solution(mesh):
    in_specs = (
        P("groups", "tok", None),
        P(("groups", "tok"), None),
        P("section", "tok", None),
        P("section", None),
    )
    out_specs = (P("section", "groups", "tok", None), P("groups"))
    return jax.shard_map(
        per_device, mesh=mesh, in_specs=in_specs, out_specs=out_specs, check_vma=False
    )
```

```python
import math

import jax
import jax.numpy as jnp
from jax import lax
from jax.sharding import PartitionSpec as P

epsilon = 1e-05
gelu_scale = math.sqrt(2.0 / math.pi)
cubic_term = 0.044715

RING_GATHER = True


def shifted(x, axis, by):
    size = lax.axis_size(axis)
    pairs = [(i, i + by) for i in range(size) if 0 <= i + by < size]
    return lax.ppermute(x, axis, pairs)


def gelu_value(pre_act):
    inner = jnp.tanh(gelu_scale * (pre_act + cubic_term * pre_act * pre_act * pre_act))
    return 0.5 * pre_act * (1.0 + inner)


def gelu_slope(pre_act):
    inner = jnp.tanh(gelu_scale * (pre_act + cubic_term * pre_act * pre_act * pre_act))
    return 0.5 * (1.0 + inner) + 0.5 * pre_act * (1.0 - inner * inner) * gelu_scale * (
        1.0 + 3.0 * cubic_term * pre_act * pre_act
    )


def section_forward(rows_in, gain, weight):
    values = rows_in.astype(jnp.float32)
    row_mean = jnp.mean(values, axis=-1, keepdims=True)
    centred = values - row_mean
    inv_std = lax.rsqrt(jnp.mean(centred * centred, axis=-1, keepdims=True) + epsilon)
    unit_rows = centred * inv_std
    normed = (unit_rows * gain).astype(jnp.bfloat16)
    pre_act = jnp.dot(normed, weight, preferred_element_type=jnp.float32)
    output = (values + gelu_value(pre_act)).astype(jnp.bfloat16)
    return (output, unit_rows, inv_std, pre_act)


def section_backward(grad_out, gain, weight, unit_rows, inv_std, slope):
    grad_pre = (grad_out * slope).astype(jnp.bfloat16)
    grad_norm = lax.dot_general(
        grad_pre, weight, (((1,), (1,)), ((), ())), preferred_element_type=jnp.float32
    )
    scaled = grad_norm * gain
    grad_in = grad_out + inv_std * (
        scaled
        - jnp.mean(scaled, axis=-1, keepdims=True)
        - unit_rows * jnp.mean(scaled * unit_rows, axis=-1, keepdims=True)
    )
    return grad_in.astype(jnp.bfloat16)


def score_terms(member_gram, member_obs, obs_sq, size):
    count = member_gram.shape[0]
    diag_vals = jnp.diagonal(member_gram)
    apart = diag_vals[:, None] + diag_vals[None, :] - 2.0 * member_gram
    same = jnp.eye(count, dtype=jnp.float32)
    others = 1.0 - same
    pair_dist = jnp.sqrt(jnp.where(same > 0.5, size, apart) / size + epsilon)
    to_obs = jnp.sqrt((diag_vals - 2.0 * member_obs + obs_sq) / size + epsilon)
    energy = jnp.mean(to_obs) - jnp.sum(others * pair_dist) / (2.0 * count * (count - 1))
    pair_coeff = others / (count * (count - 1) * pair_dist)
    obs_coeff = 1.0 / (count * to_obs)
    member_coeff = pair_coeff + same * (obs_coeff - jnp.sum(pair_coeff, axis=1))[:, None]
    return (energy, member_coeff, -obs_coeff)


def snake_ring(n):
    if n % 2:
        return list(range(n))
    return list(range(0, n, 2)) + list(range(n - 1, 0, -2))


def ring_gather(local, axis, pieces=2):
    n = lax.axis_size(axis)
    rows, cols = local.shape
    if n == 1:
        return local
    ring = snake_ring(n)
    pos_of = [0] * n
    for p, t in enumerate(ring):
        pos_of[t] = p
    me = lax.axis_index(axis)
    my_pos = jnp.asarray(pos_of, jnp.int32)[me]
    ring_arr = jnp.asarray(ring, jnp.int32)
    cw = [(ring[i], ring[(i + 1) % n]) for i in range(n)]
    ccw = [(ring[(i + 1) % n], ring[i]) for i in range(n)]
    width = cols // (2 * pieces)
    parts = [local[:, j * width:(j + 1) * width] for j in range(2 * pieces)]
    full = jnp.zeros((n * rows, cols), local.dtype)
    full = lax.dynamic_update_slice(full, local, (me * rows, 0))
    for k in range(1, n):
        from_cw = ring_arr[(my_pos - k) % n]
        from_ccw = ring_arr[(my_pos + k) % n]
        for j in range(2 * pieces):
            clockwise = j % 2 == 0
            parts[j] = lax.ppermute(parts[j], axis, cw if clockwise else ccw)
            origin = from_cw if clockwise else from_ccw
            full = lax.dynamic_update_slice(full, parts[j], (origin * rows, j * width))
    return full


def tree_sum(v, axis):
    n = lax.axis_size(axis)
    if n & (n - 1):
        return lax.psum(v, axis)
    b = 1
    while b < n:
        v = v + lax.ppermute(v, axis, [(i, i ^ b) for i in range(n)])
        b *= 2
    return v


def per_device(inputs, obs, weights, gains):
    sec = lax.axis_index("section")
    on_first = sec == 0
    gain = gains[0]
    tok_rows = obs.shape[0]
    width = obs.shape[1]
    size = float(tok_rows * lax.axis_size("tok") * width)

    obs_sq = jnp.einsum("rd,rd->", obs, obs, preferred_element_type=jnp.float32)

    if RING_GATHER:
        weight = ring_gather(weights[0], "tok")
    else:
        weight = lax.all_gather(weights, "tok", axis=1, tiled=True)[0]

    inputs, weight = lax.optimization_barrier((inputs, weight))
    members = inputs.shape[0]
    rows_all = inputs.reshape(members * tok_rows, width)

    fa = section_forward(rows_all, gain, weight)
    arrived = shifted(fa[0], "section", 1)
    fb = section_forward(arrived, gain, weight)

    y = fb[0].astype(jnp.float32).reshape(members, tok_rows, width)
    obs_f = obs.astype(jnp.float32)
    terms = []
    for m in range(members):
        for k in range(members):
            terms.append(jnp.sum(y[m] * y[k], axis=-1))
    for m in range(members):
        terms.append(jnp.sum(y[m] * obs_f, axis=-1))
    terms = jnp.sum(jnp.stack(terms), axis=-1)
    packed = tree_sum(jnp.concatenate([terms, obs_sq.reshape(1)]), "tok")
    slope_a, slope_b = lax.optimization_barrier((gelu_slope(fa[3]), gelu_slope(fb[3])))
    member_gram = packed[: members * members].reshape(members, members)
    obs_rows = packed[members * members : members * members + members]
    obs_total = packed[members * members + members]
    energy, member_coeff, obs_coeff = score_terms(member_gram, obs_rows, obs_total, size)
    energy_arr = jnp.reshape(energy, (1,))
    energy_peer = shifted(energy_arr, "section", -1)
    energy_out = jnp.where(on_first, energy_peer, energy_arr)

    cots = []
    for m in range(members):
        c = obs_coeff[m] * obs_f
        for k in range(members):
            c = c + member_coeff[m, k] * y[k]
        cots.append(c)
    cot = jnp.concatenate(cots, axis=0)

    da = section_backward(cot, gain, weight, fb[1], fb[2], slope_b)
    back = shifted(da, "section", -1)
    db = section_backward(back.astype(jnp.float32), gain, weight, fa[1], fa[2], slope_a)
    grads = jnp.where(on_first, db, da).reshape(members, tok_rows, width)
    return (grads[None], energy_out)


def solution(mesh):
    in_specs = (
        P("groups", "tok", None),
        P(("groups", "tok"), None),
        P("section", "tok", None),
        P("section", None),
    )
    out_specs = (P("section", "groups", "tok", None), P("groups"))
    return jax.shard_map(
        per_device, mesh=mesh, in_specs=in_specs, out_specs=out_specs, check_vma=False
    )
```

```python
import math

import jax
import jax.numpy as jnp
from jax import lax
from jax.sharding import PartitionSpec as P

epsilon = 1e-05
gelu_scale = math.sqrt(2.0 / math.pi)
cubic_term = 0.044715

RING_GATHER = True


def shifted(x, axis, by):
    size = lax.axis_size(axis)
    pairs = [(i, i + by) for i in range(size) if 0 <= i + by < size]
    return lax.ppermute(x, axis, pairs)


def gelu_value(pre_act):
    inner = jnp.tanh(gelu_scale * (pre_act + cubic_term * pre_act * pre_act * pre_act))
    return 0.5 * pre_act * (1.0 + inner)


def gelu_slope(pre_act):
    inner = jnp.tanh(gelu_scale * (pre_act + cubic_term * pre_act * pre_act * pre_act))
    return 0.5 * (1.0 + inner) + 0.5 * pre_act * (1.0 - inner * inner) * gelu_scale * (
        1.0 + 3.0 * cubic_term * pre_act * pre_act
    )


def section_forward(rows_in, gain, weight):
    values = rows_in.astype(jnp.float32)
    row_mean = jnp.mean(values, axis=-1, keepdims=True)
    centred = values - row_mean
    inv_std = lax.rsqrt(jnp.mean(centred * centred, axis=-1, keepdims=True) + epsilon)
    unit_rows = centred * inv_std
    normed = (unit_rows * gain).astype(jnp.bfloat16)
    pre_act = jnp.dot(normed, weight, preferred_element_type=jnp.float32)
    output = (values + gelu_value(pre_act)).astype(jnp.bfloat16)
    return (output, unit_rows, inv_std, pre_act)


def section_backward(grad_out, gain, weight, unit_rows, inv_std, slope):
    grad_pre = (grad_out * slope).astype(jnp.bfloat16)
    grad_norm = lax.dot_general(
        grad_pre, weight, (((1,), (1,)), ((), ())), preferred_element_type=jnp.float32
    )
    scaled = grad_norm * gain
    grad_in = grad_out + inv_std * (
        scaled
        - jnp.mean(scaled, axis=-1, keepdims=True)
        - unit_rows * jnp.mean(scaled * unit_rows, axis=-1, keepdims=True)
    )
    return grad_in.astype(jnp.bfloat16)


def score_terms(member_gram, member_obs, obs_sq, size):
    count = member_gram.shape[0]
    diag_vals = jnp.diagonal(member_gram)
    apart = diag_vals[:, None] + diag_vals[None, :] - 2.0 * member_gram
    same = jnp.eye(count, dtype=jnp.float32)
    others = 1.0 - same
    pair_dist = jnp.sqrt(jnp.where(same > 0.5, size, apart) / size + epsilon)
    to_obs = jnp.sqrt((diag_vals - 2.0 * member_obs + obs_sq) / size + epsilon)
    energy = jnp.mean(to_obs) - jnp.sum(others * pair_dist) / (2.0 * count * (count - 1))
    pair_coeff = others / (count * (count - 1) * pair_dist)
    obs_coeff = 1.0 / (count * to_obs)
    member_coeff = pair_coeff + same * (obs_coeff - jnp.sum(pair_coeff, axis=1))[:, None]
    return (energy, member_coeff, -obs_coeff)


def snake_ring(n):
    if n % 2:
        return list(range(n))
    return list(range(0, n, 2)) + list(range(n - 1, 0, -2))


def ring_gather(local, axis, pieces=2):
    n = lax.axis_size(axis)
    rows, cols = local.shape
    if n == 1 or n % 2:
        return lax.all_gather(local, axis, axis=0, tiled=True)
    ring = snake_ring(n)
    me = lax.axis_index(axis)
    my_pos = jnp.where(me % 2 == 0, me // 2, n - (me + 1) // 2)

    def tok_at(p):
        p = p % n
        return jnp.where(p < n // 2, 2 * p, 2 * (n - 1 - p) + 1)

    cw = [(ring[i], ring[(i + 1) % n]) for i in range(n)]
    ccw = [(ring[(i + 1) % n], ring[i]) for i in range(n)]
    width = cols // (2 * pieces)
    parts = [local[:, j * width:(j + 1) * width] for j in range(2 * pieces)]
    full = jnp.zeros((n * rows, cols), local.dtype)
    for k in range(1, n):
        from_cw = tok_at(my_pos - k + n)
        from_ccw = tok_at(my_pos + k)
        for j in range(2 * pieces):
            clockwise = j % 2 == 0
            parts[j] = lax.ppermute(parts[j], axis, cw if clockwise else ccw)
            origin = from_cw if clockwise else from_ccw
            full = lax.dynamic_update_slice(full, parts[j], (origin * rows, j * width))
    full, local = lax.optimization_barrier((full, local))
    return lax.dynamic_update_slice(full, local, (me * rows, 0))


def tree_sum(v, axis):
    n = lax.axis_size(axis)
    if n & (n - 1):
        return lax.psum(v, axis)
    b = 1
    while b < n:
        v = v + lax.ppermute(v, axis, [(i, i ^ b) for i in range(n)])
        b *= 2
    return v


def per_device(inputs, obs, weights, gains):
    sec = lax.axis_index("section")
    on_first = sec == 0
    gain = gains[0]
    tok_rows = obs.shape[0]
    width = obs.shape[1]
    size = float(tok_rows * lax.axis_size("tok") * width)

    obs_sq = jnp.einsum("rd,rd->", obs, obs, preferred_element_type=jnp.float32)

    if RING_GATHER:
        weight = ring_gather(weights[0], "tok")
    else:
        weight = lax.all_gather(weights, "tok", axis=1, tiled=True)[0]

    inputs, weight = lax.optimization_barrier((inputs, weight))
    members = inputs.shape[0]
    rows_all = inputs.reshape(members * tok_rows, width)

    fa = section_forward(rows_all, gain, weight)
    arrived = shifted(fa[0], "section", 1)
    fb = section_forward(arrived, gain, weight)

    y = fb[0].astype(jnp.float32).reshape(members, tok_rows, width)
    obs_f = obs.astype(jnp.float32)
    terms = []
    for m in range(members):
        for k in range(members):
            terms.append(jnp.sum(y[m] * y[k], axis=-1))
    for m in range(members):
        terms.append(jnp.sum(y[m] * obs_f, axis=-1))
    terms = jnp.sum(jnp.stack(terms), axis=-1)
    packed = tree_sum(jnp.concatenate([terms, obs_sq.reshape(1)]), "tok")
    slope_a, slope_b = lax.optimization_barrier((gelu_slope(fa[3]), gelu_slope(fb[3])))
    member_gram = packed[: members * members].reshape(members, members)
    obs_rows = packed[members * members : members * members + members]
    obs_total = packed[members * members + members]
    energy, member_coeff, obs_coeff = score_terms(member_gram, obs_rows, obs_total, size)
    energy_arr = jnp.reshape(energy, (1,))
    energy_peer = shifted(energy_arr, "section", -1)
    energy_out = jnp.where(on_first, energy_peer, energy_arr)

    cots = []
    for m in range(members):
        c = obs_coeff[m] * obs_f
        for k in range(members):
            c = c + member_coeff[m, k] * y[k]
        cots.append(c)
    cot = jnp.concatenate(cots, axis=0)

    da = section_backward(cot, gain, weight, fb[1], fb[2], slope_b)
    back = shifted(da, "section", -1)
    db = section_backward(back.astype(jnp.float32), gain, weight, fa[1], fa[2], slope_a)
    grads = jnp.where(on_first, db, da).reshape(members, tok_rows, width)
    return (grads[None], energy_out)


def solution(mesh):
    in_specs = (
        P("groups", "tok", None),
        P(("groups", "tok"), None),
        P("section", "tok", None),
        P("section", None),
    )
    out_specs = (P("section", "groups", "tok", None), P("groups"))
    return jax.shard_map(
        per_device, mesh=mesh, in_specs=in_specs, out_specs=out_specs, check_vma=False
    )
```

```python
import math

import jax
import jax.numpy as jnp
from jax import lax
from jax.sharding import PartitionSpec as P

epsilon = 1e-05
gelu_scale = math.sqrt(2.0 / math.pi)
cubic_term = 0.044715

RING_GATHER = True


def shifted(x, axis, by):
    size = lax.axis_size(axis)
    pairs = [(i, i + by) for i in range(size) if 0 <= i + by < size]
    return lax.ppermute(x, axis, pairs)


def gelu_value(pre_act):
    inner = jnp.tanh(gelu_scale * (pre_act + cubic_term * pre_act * pre_act * pre_act))
    return 0.5 * pre_act * (1.0 + inner)


def gelu_slope(pre_act):
    inner = jnp.tanh(gelu_scale * (pre_act + cubic_term * pre_act * pre_act * pre_act))
    return 0.5 * (1.0 + inner) + 0.5 * pre_act * (1.0 - inner * inner) * gelu_scale * (
        1.0 + 3.0 * cubic_term * pre_act * pre_act
    )


def section_forward(rows_in, gain, weight):
    values = rows_in.astype(jnp.float32)
    row_mean = jnp.mean(values, axis=-1, keepdims=True)
    centred = values - row_mean
    inv_std = lax.rsqrt(jnp.mean(centred * centred, axis=-1, keepdims=True) + epsilon)
    unit_rows = centred * inv_std
    normed = (unit_rows * gain).astype(jnp.bfloat16)
    pre_act = jnp.dot(normed, weight, preferred_element_type=jnp.float32)
    output = (values + gelu_value(pre_act)).astype(jnp.bfloat16)
    return (output, unit_rows, inv_std, pre_act)


def section_backward(grad_out, gain, weight, unit_rows, inv_std, slope):
    grad_pre = (grad_out * slope).astype(jnp.bfloat16)
    grad_norm = lax.dot_general(
        grad_pre, weight, (((1,), (1,)), ((), ())), preferred_element_type=jnp.float32
    )
    scaled = grad_norm * gain
    grad_in = grad_out + inv_std * (
        scaled
        - jnp.mean(scaled, axis=-1, keepdims=True)
        - unit_rows * jnp.mean(scaled * unit_rows, axis=-1, keepdims=True)
    )
    return grad_in.astype(jnp.bfloat16)


def score_terms(member_gram, member_obs, obs_sq, size):
    count = member_gram.shape[0]
    diag_vals = jnp.diagonal(member_gram)
    apart = diag_vals[:, None] + diag_vals[None, :] - 2.0 * member_gram
    same = jnp.eye(count, dtype=jnp.float32)
    others = 1.0 - same
    pair_dist = jnp.sqrt(jnp.where(same > 0.5, size, apart) / size + epsilon)
    to_obs = jnp.sqrt((diag_vals - 2.0 * member_obs + obs_sq) / size + epsilon)
    energy = jnp.mean(to_obs) - jnp.sum(others * pair_dist) / (2.0 * count * (count - 1))
    pair_coeff = others / (count * (count - 1) * pair_dist)
    obs_coeff = 1.0 / (count * to_obs)
    member_coeff = pair_coeff + same * (obs_coeff - jnp.sum(pair_coeff, axis=1))[:, None]
    return (energy, member_coeff, -obs_coeff)


def snake_ring(n):
    if n % 2:
        return list(range(n))
    return list(range(0, n, 2)) + list(range(n - 1, 0, -2))


def ring_gather(local, axis, pieces=2):
    n = lax.axis_size(axis)
    rows, cols = local.shape
    if n == 1 or n % 2:
        return lax.all_gather(local, axis, axis=0, tiled=True)
    ring = snake_ring(n)
    me = lax.axis_index(axis)
    my_pos = jnp.where(me % 2 == 0, me // 2, n - (me + 1) // 2)

    def tok_at(p):
        p = p % n
        return jnp.where(p < n // 2, 2 * p, 2 * (n - 1 - p) + 1)

    cw = [(ring[i], ring[(i + 1) % n]) for i in range(n)]
    ccw = [(ring[(i + 1) % n], ring[i]) for i in range(n)]
    width = cols // (2 * pieces)
    parts = [local[:, j * width:(j + 1) * width] for j in range(2 * pieces)]
    full = jnp.zeros((n * rows, cols), local.dtype)
    for k in range(1, n):
        from_cw = tok_at(my_pos - k + n)
        from_ccw = tok_at(my_pos + k)
        for j in range(2 * pieces):
            clockwise = j % 2 == 0
            parts[j] = lax.ppermute(parts[j], axis, cw if clockwise else ccw)
            origin = from_cw if clockwise else from_ccw
            full = lax.dynamic_update_slice(full, parts[j], (origin * rows, j * width))
    full, local = lax.optimization_barrier((full, local))
    return lax.dynamic_update_slice(full, local, (me * rows, 0))


def tree_sum(v, axis):
    n = lax.axis_size(axis)
    if n & (n - 1):
        return lax.psum(v, axis)
    b = 1
    while b < n:
        v = v + lax.ppermute(v, axis, [(i, i ^ b) for i in range(n)])
        b *= 2
    return v


def packed_score(packed, count, size):
    gram = [[packed[m * count + k] for k in range(count)] for m in range(count)]
    member_obs = [packed[count * count + m] for m in range(count)]
    obs_sq = packed[count * count + count]
    diag = [gram[m][m] for m in range(count)]
    to_obs = [jnp.sqrt((diag[m] - 2.0 * member_obs[m] + obs_sq) / size + epsilon) for m in range(count)]
    pair = [[None] * count for _ in range(count)]
    pair_total = 0.0
    for m in range(count):
        for k in range(count):
            if m != k:
                pair[m][k] = jnp.sqrt((diag[m] + diag[k] - 2.0 * gram[m][k]) / size + epsilon)
                pair_total = pair_total + pair[m][k]
    energy = sum(to_obs) / count - pair_total / (2.0 * count * (count - 1))
    obs_coeff = [1.0 / (count * to_obs[m]) for m in range(count)]
    rows = []
    for m in range(count):
        row = []
        off = 0.0
        for k in range(count):
            if m != k:
                c = 1.0 / (count * (count - 1) * pair[m][k])
                off = off + c
                row.append(c)
            else:
                row.append(None)
        row[m] = obs_coeff[m] - off
        rows.append(jnp.stack(row))
    return (energy, jnp.stack(rows), -jnp.stack(obs_coeff))


def per_device(inputs, obs, weights, gains):
    sec = lax.axis_index("section")
    on_first = sec == 0
    gain = gains[0]
    tok_rows = obs.shape[0]
    width = obs.shape[1]
    size = float(tok_rows * lax.axis_size("tok") * width)

    obs_sq = jnp.einsum("rd,rd->", obs, obs, preferred_element_type=jnp.float32)

    if RING_GATHER:
        weight = ring_gather(weights[0], "tok")
    else:
        weight = lax.all_gather(weights, "tok", axis=1, tiled=True)[0]

    inputs, weight = lax.optimization_barrier((inputs, weight))
    members = inputs.shape[0]
    rows_all = inputs.reshape(members * tok_rows, width)

    fa = section_forward(rows_all, gain, weight)
    arrived = shifted(fa[0], "section", 1)
    fb = section_forward(arrived, gain, weight)

    y = fb[0].reshape(members, tok_rows, width)
    obs_f = obs.astype(jnp.float32)
    yf = y.astype(jnp.float32)
    terms = []
    for m in range(members):
        for k in range(members):
            terms.append(jnp.sum(yf[m] * yf[k], axis=-1))
    for m in range(members):
        terms.append(jnp.sum(yf[m] * obs_f, axis=-1))
    terms = jnp.sum(jnp.stack(terms), axis=-1)
    packed = tree_sum(jnp.concatenate([terms, obs_sq.reshape(1)]), "tok")
    slope_a, slope_b = lax.optimization_barrier((gelu_slope(fa[3]), gelu_slope(fb[3])))
    energy, member_coeff, obs_coeff = packed_score(packed, members, size)
    energy_arr = jnp.reshape(energy, (1,))

    cot = obs_coeff[:, None, None] * obs_f[None]
    for k in range(members):
        cot = cot + member_coeff[:, k, None, None] * y[k].astype(jnp.float32)[None]
    cot = cot.reshape(members * tok_rows, width)

    da = section_backward(cot, gain, weight, fb[1], fb[2], slope_b)
    back = shifted(da, "section", -1)
    energy_arr, back = lax.optimization_barrier((energy_arr, back))
    energy_peer = shifted(energy_arr, "section", -1)
    energy_out = jnp.where(on_first, energy_peer, energy_arr)
    db = section_backward(back.astype(jnp.float32), gain, weight, fa[1], fa[2], slope_a)
    grads = jnp.where(on_first, db, da).reshape(members, tok_rows, width)
    return (grads[None], energy_out)


def solution(mesh):
    in_specs = (
        P("groups", "tok", None),
        P(("groups", "tok"), None),
        P("section", "tok", None),
        P("section", None),
    )
    out_specs = (P("section", "groups", "tok", None), P("groups"))
    return jax.shard_map(
        per_device, mesh=mesh, in_specs=in_specs, out_specs=out_specs, check_vma=False
    )
```

```python
import math

import jax
import jax.numpy as jnp
from jax import lax
from jax.sharding import PartitionSpec as P

epsilon = 1e-05
gelu_scale = math.sqrt(2.0 / math.pi)
cubic_term = 0.044715

RING_GATHER = True


def shifted(x, axis, by):
    size = lax.axis_size(axis)
    pairs = [(i, i + by) for i in range(size) if 0 <= i + by < size]
    return lax.ppermute(x, axis, pairs)


def gelu_value(pre_act):
    inner = jnp.tanh(gelu_scale * (pre_act + cubic_term * pre_act * pre_act * pre_act))
    return 0.5 * pre_act * (1.0 + inner)


def gelu_slope(pre_act):
    inner = jnp.tanh(gelu_scale * (pre_act + cubic_term * pre_act * pre_act * pre_act))
    return 0.5 * (1.0 + inner) + 0.5 * pre_act * (1.0 - inner * inner) * gelu_scale * (
        1.0 + 3.0 * cubic_term * pre_act * pre_act
    )


def section_forward(rows_in, gain, weight):
    values = rows_in.astype(jnp.float32)
    row_mean = jnp.mean(values, axis=-1, keepdims=True)
    centred = values - row_mean
    inv_std = lax.rsqrt(jnp.mean(centred * centred, axis=-1, keepdims=True) + epsilon)
    unit_rows = centred * inv_std
    normed = (unit_rows * gain).astype(jnp.bfloat16)
    pre_act = jnp.dot(normed, weight, preferred_element_type=jnp.float32)
    output = (values + gelu_value(pre_act)).astype(jnp.bfloat16)
    return (output, unit_rows, inv_std, pre_act)


def section_backward(grad_out, gain, weight, unit_rows, inv_std, slope):
    grad_pre = (grad_out * slope).astype(jnp.bfloat16)
    grad_norm = lax.dot_general(
        grad_pre, weight, (((1,), (1,)), ((), ())), preferred_element_type=jnp.float32
    )
    scaled = grad_norm * gain
    grad_in = grad_out + inv_std * (
        scaled
        - jnp.mean(scaled, axis=-1, keepdims=True)
        - unit_rows * jnp.mean(scaled * unit_rows, axis=-1, keepdims=True)
    )
    return grad_in.astype(jnp.bfloat16)


def score_terms(member_gram, member_obs, obs_sq, size):
    count = member_gram.shape[0]
    diag_vals = jnp.diagonal(member_gram)
    apart = diag_vals[:, None] + diag_vals[None, :] - 2.0 * member_gram
    same = jnp.eye(count, dtype=jnp.float32)
    others = 1.0 - same
    pair_dist = jnp.sqrt(jnp.where(same > 0.5, size, apart) / size + epsilon)
    to_obs = jnp.sqrt((diag_vals - 2.0 * member_obs + obs_sq) / size + epsilon)
    energy = jnp.mean(to_obs) - jnp.sum(others * pair_dist) / (2.0 * count * (count - 1))
    pair_coeff = others / (count * (count - 1) * pair_dist)
    obs_coeff = 1.0 / (count * to_obs)
    member_coeff = pair_coeff + same * (obs_coeff - jnp.sum(pair_coeff, axis=1))[:, None]
    return (energy, member_coeff, -obs_coeff)


def snake_ring(n):
    if n % 2:
        return list(range(n))
    return list(range(0, n, 2)) + list(range(n - 1, 0, -2))


def ring_gather(local, axis, pieces=2):
    n = lax.axis_size(axis)
    rows, cols = local.shape
    if n == 1 or n % 2:
        return lax.all_gather(local, axis, axis=0, tiled=True)
    ring = snake_ring(n)
    me = lax.axis_index(axis)
    my_pos = jnp.where(me % 2 == 0, me // 2, n - (me + 1) // 2)

    def tok_at(p):
        p = p % n
        return jnp.where(p < n // 2, 2 * p, 2 * (n - 1 - p) + 1)

    cw = [(ring[i], ring[(i + 1) % n]) for i in range(n)]
    ccw = [(ring[(i + 1) % n], ring[i]) for i in range(n)]
    width = cols // (2 * pieces)
    parts = [local[:, j * width:(j + 1) * width] for j in range(2 * pieces)]
    full = jnp.zeros((n * rows, cols), local.dtype)
    for k in range(1, n):
        from_cw = tok_at(my_pos - k + n)
        from_ccw = tok_at(my_pos + k)
        for j in range(2 * pieces):
            clockwise = j % 2 == 0
            parts[j] = lax.ppermute(parts[j], axis, cw if clockwise else ccw)
            origin = from_cw if clockwise else from_ccw
            full = lax.dynamic_update_slice(full, parts[j], (origin * rows, j * width))
    full, local = lax.optimization_barrier((full, local))
    return lax.dynamic_update_slice(full, local, (me * rows, 0))


def ring_gather_shared(local, axis, pair_axis):
    n = lax.axis_size(axis)
    rows, cols = local.shape
    w = cols // 8
    ring = snake_ring(n)
    me = lax.axis_index(axis)
    g = lax.axis_index(pair_axis)
    my_pos = jnp.where(me % 2 == 0, me // 2, n - (me + 1) // 2)

    def tok_at(p):
        p = p % n
        return jnp.where(p < n // 2, 2 * p, 2 * (n - 1 - p) + 1)

    def col_of(j, plane):
        return jnp.where(plane == 0, j * w, cols - (j + 1) * w)

    cw = [(ring[i], ring[(i + 1) % n]) for i in range(n)]
    ccw = [(ring[(i + 1) % n], ring[i]) for i in range(n)]
    swap = [(0, 1), (1, 0)]
    parts = [lax.dynamic_slice(local, (0, col_of(j, g)), (rows, w)) for j in range(6)]
    full = jnp.zeros((n * rows, cols), local.dtype)
    swapped = {}
    for k in range(1, n):
        if k - 2 in swapped:
            parts, swapped[k - 2] = lax.optimization_barrier((parts, swapped[k - 2]))
        from_cw = tok_at(my_pos - k + n)
        from_ccw = tok_at(my_pos + k)
        for j in range(6):
            clockwise = j % 2 == 0
            parts[j] = lax.ppermute(parts[j], axis, cw if clockwise else ccw)
            origin = from_cw if clockwise else from_ccw
            full = lax.dynamic_update_slice(full, parts[j], (origin * rows, col_of(j, g)))
        swapped[k] = (
            [lax.ppermute(parts[j], pair_axis, swap) for j in range(2)],
            [from_cw, from_ccw],
        )
    for k in range(1, n):
        pieces, origins = swapped[k]
        for j in range(2):
            full = lax.dynamic_update_slice(full, pieces[j], (origins[j] * rows, col_of(j, 1 - g)))
    full, local = lax.optimization_barrier((full, local))
    return lax.dynamic_update_slice(full, local, (me * rows, 0))


def tree_sum(v, axis):
    n = lax.axis_size(axis)
    if n & (n - 1):
        return lax.psum(v, axis)
    b = 1
    while b < n:
        v = v + lax.ppermute(v, axis, [(i, i ^ b) for i in range(n)])
        b *= 2
    return v


def packed_score(packed, count, size):
    gram = [[packed[m * count + k] for k in range(count)] for m in range(count)]
    member_obs = [packed[count * count + m] for m in range(count)]
    obs_sq = packed[count * count + count]
    diag = [gram[m][m] for m in range(count)]
    to_obs = [jnp.sqrt((diag[m] - 2.0 * member_obs[m] + obs_sq) / size + epsilon) for m in range(count)]
    pair = [[None] * count for _ in range(count)]
    pair_total = 0.0
    for m in range(count):
        for k in range(count):
            if m != k:
                pair[m][k] = jnp.sqrt((diag[m] + diag[k] - 2.0 * gram[m][k]) / size + epsilon)
                pair_total = pair_total + pair[m][k]
    energy = sum(to_obs) / count - pair_total / (2.0 * count * (count - 1))
    obs_coeff = [1.0 / (count * to_obs[m]) for m in range(count)]
    rows = []
    for m in range(count):
        row = []
        off = 0.0
        for k in range(count):
            if m != k:
                c = 1.0 / (count * (count - 1) * pair[m][k])
                off = off + c
                row.append(c)
            else:
                row.append(None)
        row[m] = obs_coeff[m] - off
        rows.append(jnp.stack(row))
    return (energy, jnp.stack(rows), -jnp.stack(obs_coeff))


def per_device(inputs, obs, weights, gains):
    sec = lax.axis_index("section")
    on_first = sec == 0
    gain = gains[0]
    tok_rows = obs.shape[0]
    width = obs.shape[1]
    size = float(tok_rows * lax.axis_size("tok") * width)

    obs_sq = jnp.einsum("rd,rd->", obs, obs, preferred_element_type=jnp.float32)

    n_tok = lax.axis_size("tok")
    shareable = (
        lax.axis_size("groups") == 2 and n_tok % 2 == 0 and 2 < n_tok <= 16
        and weights.shape[2] % 1024 == 0
    )
    if RING_GATHER and shareable:
        weight = ring_gather_shared(weights[0], "tok", "groups")
    elif RING_GATHER:
        weight = ring_gather(weights[0], "tok")
    else:
        weight = lax.all_gather(weights, "tok", axis=1, tiled=True)[0]

    inputs, weight = lax.optimization_barrier((inputs, weight))
    members = inputs.shape[0]
    rows_all = inputs.reshape(members * tok_rows, width)

    fa = section_forward(rows_all, gain, weight)
    arrived = shifted(fa[0], "section", 1)
    fb = section_forward(arrived, gain, weight)

    y = fb[0].reshape(members, tok_rows, width)
    obs_f = obs.astype(jnp.float32)
    yf = y.astype(jnp.float32)
    terms = []
    for m in range(members):
        for k in range(members):
            terms.append(jnp.sum(yf[m] * yf[k], axis=-1))
    for m in range(members):
        terms.append(jnp.sum(yf[m] * obs_f, axis=-1))
    terms = jnp.sum(jnp.stack(terms), axis=-1)
    packed = tree_sum(jnp.concatenate([terms, obs_sq.reshape(1)]), "tok")
    slope_a, slope_b = lax.optimization_barrier((gelu_slope(fa[3]), gelu_slope(fb[3])))
    energy, member_coeff, obs_coeff = packed_score(packed, members, size)
    energy_arr = jnp.reshape(energy, (1,))

    cot = obs_coeff[:, None, None] * obs_f[None]
    for k in range(members):
        cot = cot + member_coeff[:, k, None, None] * y[k].astype(jnp.float32)[None]
    cot = cot.reshape(members * tok_rows, width)

    da = section_backward(cot, gain, weight, fb[1], fb[2], slope_b)
    back = shifted(da, "section", -1)
    energy_arr, back = lax.optimization_barrier((energy_arr, back))
    energy_peer = shifted(energy_arr, "section", -1)
    energy_out = jnp.where(on_first, energy_peer, energy_arr)
    db = section_backward(back.astype(jnp.float32), gain, weight, fa[1], fa[2], slope_a)
    grads = jnp.where(on_first, db, da).reshape(members, tok_rows, width)
    return (grads[None], energy_out)


def solution(mesh):
    in_specs = (
        P("groups", "tok", None),
        P(("groups", "tok"), None),
        P("section", "tok", None),
        P("section", None),
    )
    out_specs = (P("section", "groups", "tok", None), P("groups"))
    return jax.shard_map(
        per_device, mesh=mesh, in_specs=in_specs, out_specs=out_specs, check_vma=False
    )
```

```python
import math

import jax
import jax.numpy as jnp
from jax import lax
from jax.sharding import PartitionSpec as P

epsilon = 1e-05
gelu_scale = math.sqrt(2.0 / math.pi)
cubic_term = 0.044715

RING_GATHER = True


def shifted(x, axis, by):
    size = lax.axis_size(axis)
    pairs = [(i, i + by) for i in range(size) if 0 <= i + by < size]
    return lax.ppermute(x, axis, pairs)


def gelu_value(pre_act):
    inner = jnp.tanh(gelu_scale * (pre_act + cubic_term * pre_act * pre_act * pre_act))
    return 0.5 * pre_act * (1.0 + inner)


def gelu_slope(pre_act):
    inner = jnp.tanh(gelu_scale * (pre_act + cubic_term * pre_act * pre_act * pre_act))
    return 0.5 * (1.0 + inner) + 0.5 * pre_act * (1.0 - inner * inner) * gelu_scale * (
        1.0 + 3.0 * cubic_term * pre_act * pre_act
    )


def norm_part(rows_in, gain):
    values = rows_in.astype(jnp.float32)
    row_mean = jnp.mean(values, axis=-1, keepdims=True)
    centred = values - row_mean
    inv_std = lax.rsqrt(jnp.mean(centred * centred, axis=-1, keepdims=True) + epsilon)
    unit_rows = centred * inv_std
    normed = (unit_rows * gain).astype(jnp.bfloat16)
    return (values, unit_rows, inv_std, normed)


def section_forward(rows_in, gain, weight):
    values = rows_in.astype(jnp.float32)
    row_mean = jnp.mean(values, axis=-1, keepdims=True)
    centred = values - row_mean
    inv_std = lax.rsqrt(jnp.mean(centred * centred, axis=-1, keepdims=True) + epsilon)
    unit_rows = centred * inv_std
    normed = (unit_rows * gain).astype(jnp.bfloat16)
    pre_act = jnp.dot(normed, weight, preferred_element_type=jnp.float32)
    output = (values + gelu_value(pre_act)).astype(jnp.bfloat16)
    return (output, unit_rows, inv_std, pre_act)


def section_backward(grad_out, gain, weight, unit_rows, inv_std, slope):
    grad_pre = (grad_out * slope).astype(jnp.bfloat16)
    grad_norm = lax.dot_general(
        grad_pre, weight, (((1,), (1,)), ((), ())), preferred_element_type=jnp.float32
    )
    scaled = grad_norm * gain
    grad_in = grad_out + inv_std * (
        scaled
        - jnp.mean(scaled, axis=-1, keepdims=True)
        - unit_rows * jnp.mean(scaled * unit_rows, axis=-1, keepdims=True)
    )
    return grad_in.astype(jnp.bfloat16)


def score_terms(member_gram, member_obs, obs_sq, size):
    count = member_gram.shape[0]
    diag_vals = jnp.diagonal(member_gram)
    apart = diag_vals[:, None] + diag_vals[None, :] - 2.0 * member_gram
    same = jnp.eye(count, dtype=jnp.float32)
    others = 1.0 - same
    pair_dist = jnp.sqrt(jnp.where(same > 0.5, size, apart) / size + epsilon)
    to_obs = jnp.sqrt((diag_vals - 2.0 * member_obs + obs_sq) / size + epsilon)
    energy = jnp.mean(to_obs) - jnp.sum(others * pair_dist) / (2.0 * count * (count - 1))
    pair_coeff = others / (count * (count - 1) * pair_dist)
    obs_coeff = 1.0 / (count * to_obs)
    member_coeff = pair_coeff + same * (obs_coeff - jnp.sum(pair_coeff, axis=1))[:, None]
    return (energy, member_coeff, -obs_coeff)


def snake_ring(n):
    if n % 2:
        return list(range(n))
    return list(range(0, n, 2)) + list(range(n - 1, 0, -2))


def ring_gather(local, axis, pieces=2, on_piece=None):
    n = lax.axis_size(axis)
    rows, cols = local.shape
    if n == 1 or n % 2:
        return lax.all_gather(local, axis, axis=0, tiled=True)
    ring = snake_ring(n)
    me = lax.axis_index(axis)
    my_pos = jnp.where(me % 2 == 0, me // 2, n - (me + 1) // 2)

    def tok_at(p):
        p = p % n
        return jnp.where(p < n // 2, 2 * p, 2 * (n - 1 - p) + 1)

    cw = [(ring[i], ring[(i + 1) % n]) for i in range(n)]
    ccw = [(ring[(i + 1) % n], ring[i]) for i in range(n)]
    width = cols // (2 * pieces)
    parts = [local[:, j * width:(j + 1) * width] for j in range(2 * pieces)]
    full = jnp.zeros((n * rows, cols), local.dtype)
    for k in range(1, n):
        from_cw = tok_at(my_pos - k + n)
        from_ccw = tok_at(my_pos + k)
        for j in range(2 * pieces):
            clockwise = j % 2 == 0
            parts[j] = lax.ppermute(parts[j], axis, cw if clockwise else ccw)
            origin = from_cw if clockwise else from_ccw
            full = lax.dynamic_update_slice(full, parts[j], (origin * rows, j * width))
            if on_piece is not None:
                on_piece(origin, j, parts[j])
    full, local = lax.optimization_barrier((full, local))
    return lax.dynamic_update_slice(full, local, (me * rows, 0))


def tree_sum(v, axis):
    n = lax.axis_size(axis)
    if n & (n - 1):
        return lax.psum(v, axis)
    b = 1
    while b < n:
        v = v + lax.ppermute(v, axis, [(i, i ^ b) for i in range(n)])
        b *= 2
    return v


def packed_score(packed, count, size):
    gram = [[packed[m * count + k] for k in range(count)] for m in range(count)]
    member_obs = [packed[count * count + m] for m in range(count)]
    obs_sq = packed[count * count + count]
    diag = [gram[m][m] for m in range(count)]
    to_obs = [jnp.sqrt((diag[m] - 2.0 * member_obs[m] + obs_sq) / size + epsilon) for m in range(count)]
    pair = [[None] * count for _ in range(count)]
    pair_total = 0.0
    for m in range(count):
        for k in range(count):
            if m != k:
                pair[m][k] = jnp.sqrt((diag[m] + diag[k] - 2.0 * gram[m][k]) / size + epsilon)
                pair_total = pair_total + pair[m][k]
    energy = sum(to_obs) / count - pair_total / (2.0 * count * (count - 1))
    obs_coeff = [1.0 / (count * to_obs[m]) for m in range(count)]
    rows = []
    for m in range(count):
        row = []
        off = 0.0
        for k in range(count):
            if m != k:
                c = 1.0 / (count * (count - 1) * pair[m][k])
                off = off + c
                row.append(c)
            else:
                row.append(None)
        row[m] = obs_coeff[m] - off
        rows.append(jnp.stack(row))
    return (energy, jnp.stack(rows), -jnp.stack(obs_coeff))


def per_device(inputs, obs, weights, gains):
    sec = lax.axis_index("section")
    on_first = sec == 0
    gain = gains[0]
    tok_rows = obs.shape[0]
    width = obs.shape[1]
    size = float(tok_rows * lax.axis_size("tok") * width)

    obs_sq = jnp.einsum("rd,rd->", obs, obs, preferred_element_type=jnp.float32)

    members = inputs.shape[0]
    rows_all = inputs.reshape(members * tok_rows, width)
    n_tok = lax.axis_size("tok")
    local = weights[0]
    rows_w = local.shape[0]
    pieces = 2
    piece_w = width // (2 * pieces)
    overlap = RING_GATHER and n_tok % 2 == 0 and 2 < n_tok <= 16

    if overlap:
        values_a, unit_a, std_a, normed_a = norm_part(rows_all, gain)
        acc = [None] * (2 * pieces)

        def on_piece(origin, j, piece):
            lhs = lax.dynamic_slice(normed_a, (0, origin * rows_w), (normed_a.shape[0], rows_w))
            term = jnp.dot(lhs, piece, preferred_element_type=jnp.float32)
            acc[j] = term if acc[j] is None else acc[j] + term

        weight = ring_gather(local, "tok", pieces, on_piece)
        me = lax.axis_index("tok")
        lhs = lax.dynamic_slice(normed_a, (0, me * rows_w), (normed_a.shape[0], rows_w))
        for j in range(2 * pieces):
            acc[j] = acc[j] + jnp.dot(
                lhs, local[:, j * piece_w:(j + 1) * piece_w], preferred_element_type=jnp.float32
            )
        pre_a = jnp.concatenate(acc, axis=1)
        out_a = (values_a + gelu_value(pre_a)).astype(jnp.bfloat16)
        fa = (out_a, unit_a, std_a, pre_a)
    else:
        if RING_GATHER:
            weight = ring_gather(local, "tok")
        else:
            weight = lax.all_gather(weights, "tok", axis=1, tiled=True)[0]
        inputs, weight = lax.optimization_barrier((inputs, weight))
        rows_all = inputs.reshape(members * tok_rows, width)
        fa = section_forward(rows_all, gain, weight)
    arrived = shifted(fa[0], "section", 1)
    fb = section_forward(arrived, gain, weight)

    y = fb[0].reshape(members, tok_rows, width)
    obs_f = obs.astype(jnp.float32)
    yf = y.astype(jnp.float32)
    terms = []
    for m in range(members):
        for k in range(members):
            terms.append(jnp.sum(yf[m] * yf[k], axis=-1))
    for m in range(members):
        terms.append(jnp.sum(yf[m] * obs_f, axis=-1))
    terms = jnp.sum(jnp.stack(terms), axis=-1)
    packed = tree_sum(jnp.concatenate([terms, obs_sq.reshape(1)]), "tok")
    slope_a, slope_b = lax.optimization_barrier((gelu_slope(fa[3]), gelu_slope(fb[3])))
    energy, member_coeff, obs_coeff = packed_score(packed, members, size)
    energy_arr = jnp.reshape(energy, (1,))

    cot = obs_coeff[:, None, None] * obs_f[None]
    for k in range(members):
        cot = cot + member_coeff[:, k, None, None] * y[k].astype(jnp.float32)[None]
    cot = cot.reshape(members * tok_rows, width)

    da = section_backward(cot, gain, weight, fb[1], fb[2], slope_b)
    back = shifted(da, "section", -1)
    energy_arr, back = lax.optimization_barrier((energy_arr, back))
    energy_peer = shifted(energy_arr, "section", -1)
    energy_out = jnp.where(on_first, energy_peer, energy_arr)
    db = section_backward(back.astype(jnp.float32), gain, weight, fa[1], fa[2], slope_a)
    grads = jnp.where(on_first, db, da).reshape(members, tok_rows, width)
    return (grads[None], energy_out)


def solution(mesh):
    in_specs = (
        P("groups", "tok", None),
        P(("groups", "tok"), None),
        P("section", "tok", None),
        P("section", None),
    )
    out_specs = (P("section", "groups", "tok", None), P("groups"))
    return jax.shard_map(
        per_device, mesh=mesh, in_specs=in_specs, out_specs=out_specs, check_vma=False
    )
```

```python
import math

import jax
import jax.numpy as jnp
from jax import lax
from jax.sharding import PartitionSpec as P

epsilon = 1e-05
gelu_scale = math.sqrt(2.0 / math.pi)
cubic_term = 0.044715

RING_GATHER = True


def shifted(x, axis, by):
    size = lax.axis_size(axis)
    pairs = [(i, i + by) for i in range(size) if 0 <= i + by < size]
    return lax.ppermute(x, axis, pairs)


def gelu_value(pre_act):
    inner = jnp.tanh(gelu_scale * (pre_act + cubic_term * pre_act * pre_act * pre_act))
    return 0.5 * pre_act * (1.0 + inner)


def gelu_slope(pre_act):
    inner = jnp.tanh(gelu_scale * (pre_act + cubic_term * pre_act * pre_act * pre_act))
    return 0.5 * (1.0 + inner) + 0.5 * pre_act * (1.0 - inner * inner) * gelu_scale * (
        1.0 + 3.0 * cubic_term * pre_act * pre_act
    )


def norm_part(rows_in, gain):
    values = rows_in.astype(jnp.float32)
    row_mean = jnp.mean(values, axis=-1, keepdims=True)
    centred = values - row_mean
    inv_std = lax.rsqrt(jnp.mean(centred * centred, axis=-1, keepdims=True) + epsilon)
    unit_rows = centred * inv_std
    normed = (unit_rows * gain).astype(jnp.bfloat16)
    return (values, unit_rows, inv_std, normed)


def section_forward(rows_in, gain, weight):
    values = rows_in.astype(jnp.float32)
    row_mean = jnp.mean(values, axis=-1, keepdims=True)
    centred = values - row_mean
    inv_std = lax.rsqrt(jnp.mean(centred * centred, axis=-1, keepdims=True) + epsilon)
    unit_rows = centred * inv_std
    normed = (unit_rows * gain).astype(jnp.bfloat16)
    pre_act = jnp.dot(normed, weight, preferred_element_type=jnp.float32)
    output = (values + gelu_value(pre_act)).astype(jnp.bfloat16)
    return (output, unit_rows, inv_std, pre_act)


def section_backward(grad_out, gain, weight, unit_rows, inv_std, slope):
    grad_pre = (grad_out * slope).astype(jnp.bfloat16)
    grad_norm = lax.dot_general(
        grad_pre, weight, (((1,), (1,)), ((), ())), preferred_element_type=jnp.float32
    )
    scaled = grad_norm * gain
    grad_in = grad_out + inv_std * (
        scaled
        - jnp.mean(scaled, axis=-1, keepdims=True)
        - unit_rows * jnp.mean(scaled * unit_rows, axis=-1, keepdims=True)
    )
    return grad_in.astype(jnp.bfloat16)


def score_terms(member_gram, member_obs, obs_sq, size):
    count = member_gram.shape[0]
    diag_vals = jnp.diagonal(member_gram)
    apart = diag_vals[:, None] + diag_vals[None, :] - 2.0 * member_gram
    same = jnp.eye(count, dtype=jnp.float32)
    others = 1.0 - same
    pair_dist = jnp.sqrt(jnp.where(same > 0.5, size, apart) / size + epsilon)
    to_obs = jnp.sqrt((diag_vals - 2.0 * member_obs + obs_sq) / size + epsilon)
    energy = jnp.mean(to_obs) - jnp.sum(others * pair_dist) / (2.0 * count * (count - 1))
    pair_coeff = others / (count * (count - 1) * pair_dist)
    obs_coeff = 1.0 / (count * to_obs)
    member_coeff = pair_coeff + same * (obs_coeff - jnp.sum(pair_coeff, axis=1))[:, None]
    return (energy, member_coeff, -obs_coeff)


def snake_ring(n):
    if n % 2:
        return list(range(n))
    return list(range(0, n, 2)) + list(range(n - 1, 0, -2))


def ring_gather(local, axis, pieces=2, on_piece=None):
    n = lax.axis_size(axis)
    rows, cols = local.shape
    if n == 1 or n % 2:
        return lax.all_gather(local, axis, axis=0, tiled=True)
    ring = snake_ring(n)
    me = lax.axis_index(axis)
    my_pos = jnp.where(me % 2 == 0, me // 2, n - (me + 1) // 2)

    def tok_at(p):
        p = p % n
        return jnp.where(p < n // 2, 2 * p, 2 * (n - 1 - p) + 1)

    cw = [(ring[i], ring[(i + 1) % n]) for i in range(n)]
    ccw = [(ring[(i + 1) % n], ring[i]) for i in range(n)]
    width = cols // (2 * pieces)
    parts = [local[:, j * width:(j + 1) * width] for j in range(2 * pieces)]
    full = jnp.zeros((n * rows, cols), local.dtype)
    for k in range(1, n):
        from_cw = tok_at(my_pos - k + n)
        from_ccw = tok_at(my_pos + k)
        for j in range(2 * pieces):
            clockwise = j % 2 == 0
            parts[j] = lax.ppermute(parts[j], axis, cw if clockwise else ccw)
            origin = from_cw if clockwise else from_ccw
            full = lax.dynamic_update_slice(full, parts[j], (origin * rows, j * width))
            if on_piece is not None:
                on_piece(origin, j, parts[j])
    full, local = lax.optimization_barrier((full, local))
    return lax.dynamic_update_slice(full, local, (me * rows, 0))


def tree_sum(v, axis):
    n = lax.axis_size(axis)
    if n & (n - 1):
        return lax.psum(v, axis)
    b = 1
    while b < n:
        v = v + lax.ppermute(v, axis, [(i, i ^ b) for i in range(n)])
        b *= 2
    return v


def packed_score(packed, count, size):
    gram = [[packed[m * count + k] for k in range(count)] for m in range(count)]
    member_obs = [packed[count * count + m] for m in range(count)]
    obs_sq = packed[count * count + count]
    diag = [gram[m][m] for m in range(count)]
    to_obs = [jnp.sqrt((diag[m] - 2.0 * member_obs[m] + obs_sq) / size + epsilon) for m in range(count)]
    pair = [[None] * count for _ in range(count)]
    pair_total = 0.0
    for m in range(count):
        for k in range(count):
            if m != k:
                pair[m][k] = jnp.sqrt((diag[m] + diag[k] - 2.0 * gram[m][k]) / size + epsilon)
                pair_total = pair_total + pair[m][k]
    energy = sum(to_obs) / count - pair_total / (2.0 * count * (count - 1))
    obs_coeff = [1.0 / (count * to_obs[m]) for m in range(count)]
    rows = []
    for m in range(count):
        row = []
        off = 0.0
        for k in range(count):
            if m != k:
                c = 1.0 / (count * (count - 1) * pair[m][k])
                off = off + c
                row.append(c)
            else:
                row.append(None)
        row[m] = obs_coeff[m] - off
        rows.append(jnp.stack(row))
    return (energy, jnp.stack(rows), -jnp.stack(obs_coeff))


def per_device(inputs, obs, weights, gains):
    sec = lax.axis_index("section")
    on_first = sec == 0
    gain = gains[0]
    tok_rows = obs.shape[0]
    width = obs.shape[1]
    size = float(tok_rows * lax.axis_size("tok") * width)

    obs_sq = jnp.einsum("rd,rd->", obs, obs, preferred_element_type=jnp.float32)

    members = inputs.shape[0]
    rows_all = inputs.reshape(members * tok_rows, width)
    n_tok = lax.axis_size("tok")
    local = weights[0]
    rows_w = local.shape[0]
    pieces = 2
    piece_w = width // (2 * pieces)
    overlap = RING_GATHER and n_tok % 2 == 0 and 2 < n_tok <= 16

    if overlap:
        acc = [None] * (2 * pieces)
        normed = []

        def on_piece(origin, j, piece):
            if not normed:
                rows_in, piece = lax.optimization_barrier((rows_all, piece))
                normed.append(norm_part(rows_in, gain))
            normed_a = normed[0][3]
            lhs = lax.dynamic_slice(normed_a, (0, origin * rows_w), (normed_a.shape[0], rows_w))
            term = jnp.dot(lhs, piece, preferred_element_type=jnp.float32)
            acc[j] = term if acc[j] is None else acc[j] + term

        weight = ring_gather(local, "tok", pieces, on_piece)
        values_a, unit_a, std_a, normed_a = normed[0]
        me = lax.axis_index("tok")
        lhs = lax.dynamic_slice(normed_a, (0, me * rows_w), (normed_a.shape[0], rows_w))
        for j in range(2 * pieces):
            acc[j] = acc[j] + jnp.dot(
                lhs, local[:, j * piece_w:(j + 1) * piece_w], preferred_element_type=jnp.float32
            )
        pre_a = jnp.concatenate(acc, axis=1)
        out_a = (values_a + gelu_value(pre_a)).astype(jnp.bfloat16)
        fa = (out_a, unit_a, std_a, pre_a)
    else:
        if RING_GATHER:
            weight = ring_gather(local, "tok")
        else:
            weight = lax.all_gather(weights, "tok", axis=1, tiled=True)[0]
        inputs, weight = lax.optimization_barrier((inputs, weight))
        rows_all = inputs.reshape(members * tok_rows, width)
        fa = section_forward(rows_all, gain, weight)
    arrived = shifted(fa[0], "section", 1)
    fb = section_forward(arrived, gain, weight)

    y = fb[0].reshape(members, tok_rows, width)
    obs_f = obs.astype(jnp.float32)
    yf = y.astype(jnp.float32)
    terms = []
    for m in range(members):
        for k in range(members):
            terms.append(jnp.sum(yf[m] * yf[k], axis=-1))
    for m in range(members):
        terms.append(jnp.sum(yf[m] * obs_f, axis=-1))
    terms = jnp.sum(jnp.stack(terms), axis=-1)
    packed = tree_sum(jnp.concatenate([terms, obs_sq.reshape(1)]), "tok")
    slope_a, slope_b = lax.optimization_barrier((gelu_slope(fa[3]), gelu_slope(fb[3])))
    energy, member_coeff, obs_coeff = packed_score(packed, members, size)
    energy_arr = jnp.reshape(energy, (1,))

    cot = obs_coeff[:, None, None] * obs_f[None]
    for k in range(members):
        cot = cot + member_coeff[:, k, None, None] * y[k].astype(jnp.float32)[None]
    cot = cot.reshape(members * tok_rows, width)

    da = section_backward(cot, gain, weight, fb[1], fb[2], slope_b)
    back = shifted(da, "section", -1)
    energy_arr, back = lax.optimization_barrier((energy_arr, back))
    energy_peer = shifted(energy_arr, "section", -1)
    energy_out = jnp.where(on_first, energy_peer, energy_arr)
    db = section_backward(back.astype(jnp.float32), gain, weight, fa[1], fa[2], slope_a)
    grads = jnp.where(on_first, db, da).reshape(members, tok_rows, width)
    return (grads[None], energy_out)


def solution(mesh):
    in_specs = (
        P("groups", "tok", None),
        P(("groups", "tok"), None),
        P("section", "tok", None),
        P("section", None),
    )
    out_specs = (P("section", "groups", "tok", None), P("groups"))
    return jax.shard_map(
        per_device, mesh=mesh, in_specs=in_specs, out_specs=out_specs, check_vma=False
    )
```

```python
import math

import jax
import jax.numpy as jnp
from jax import lax
from jax.sharding import PartitionSpec as P

epsilon = 1e-05
gelu_scale = math.sqrt(2.0 / math.pi)
cubic_term = 0.044715

RING_GATHER = True


def shifted(x, axis, by):
    size = lax.axis_size(axis)
    pairs = [(i, i + by) for i in range(size) if 0 <= i + by < size]
    return lax.ppermute(x, axis, pairs)


def gelu_value(pre_act):
    inner = jnp.tanh(gelu_scale * (pre_act + cubic_term * pre_act * pre_act * pre_act))
    return 0.5 * pre_act * (1.0 + inner)


def gelu_slope(pre_act):
    inner = jnp.tanh(gelu_scale * (pre_act + cubic_term * pre_act * pre_act * pre_act))
    return 0.5 * (1.0 + inner) + 0.5 * pre_act * (1.0 - inner * inner) * gelu_scale * (
        1.0 + 3.0 * cubic_term * pre_act * pre_act
    )


def norm_part(rows_in, gain):
    values = rows_in.astype(jnp.float32)
    row_mean = jnp.mean(values, axis=-1, keepdims=True)
    centred = values - row_mean
    inv_std = lax.rsqrt(jnp.mean(centred * centred, axis=-1, keepdims=True) + epsilon)
    unit_rows = centred * inv_std
    normed = (unit_rows * gain).astype(jnp.bfloat16)
    return (values, unit_rows, inv_std, normed)


def section_forward(rows_in, gain, weight):
    values = rows_in.astype(jnp.float32)
    row_mean = jnp.mean(values, axis=-1, keepdims=True)
    centred = values - row_mean
    inv_std = lax.rsqrt(jnp.mean(centred * centred, axis=-1, keepdims=True) + epsilon)
    unit_rows = centred * inv_std
    normed = (unit_rows * gain).astype(jnp.bfloat16)
    pre_act = jnp.dot(normed, weight, preferred_element_type=jnp.float32)
    output = (values + gelu_value(pre_act)).astype(jnp.bfloat16)
    return (output, unit_rows, inv_std, pre_act)


def section_backward(grad_out, gain, weight, unit_rows, inv_std, slope):
    grad_pre = (grad_out * slope).astype(jnp.bfloat16)
    grad_norm = lax.dot_general(
        grad_pre, weight, (((1,), (1,)), ((), ())), preferred_element_type=jnp.float32
    )
    scaled = grad_norm * gain
    grad_in = grad_out + inv_std * (
        scaled
        - jnp.mean(scaled, axis=-1, keepdims=True)
        - unit_rows * jnp.mean(scaled * unit_rows, axis=-1, keepdims=True)
    )
    return grad_in.astype(jnp.bfloat16)


def score_terms(member_gram, member_obs, obs_sq, size):
    count = member_gram.shape[0]
    diag_vals = jnp.diagonal(member_gram)
    apart = diag_vals[:, None] + diag_vals[None, :] - 2.0 * member_gram
    same = jnp.eye(count, dtype=jnp.float32)
    others = 1.0 - same
    pair_dist = jnp.sqrt(jnp.where(same > 0.5, size, apart) / size + epsilon)
    to_obs = jnp.sqrt((diag_vals - 2.0 * member_obs + obs_sq) / size + epsilon)
    energy = jnp.mean(to_obs) - jnp.sum(others * pair_dist) / (2.0 * count * (count - 1))
    pair_coeff = others / (count * (count - 1) * pair_dist)
    obs_coeff = 1.0 / (count * to_obs)
    member_coeff = pair_coeff + same * (obs_coeff - jnp.sum(pair_coeff, axis=1))[:, None]
    return (energy, member_coeff, -obs_coeff)


def snake_ring(n):
    if n % 2:
        return list(range(n))
    return list(range(0, n, 2)) + list(range(n - 1, 0, -2))


def ring_gather(local, axis, pieces=2, on_piece=None):
    n = lax.axis_size(axis)
    rows, cols = local.shape
    if n == 1 or n % 2:
        return lax.all_gather(local, axis, axis=0, tiled=True)
    ring = snake_ring(n)
    me = lax.axis_index(axis)
    my_pos = jnp.where(me % 2 == 0, me // 2, n - (me + 1) // 2)

    def tok_at(p):
        p = p % n
        return jnp.where(p < n // 2, 2 * p, 2 * (n - 1 - p) + 1)

    cw = [(ring[i], ring[(i + 1) % n]) for i in range(n)]
    ccw = [(ring[(i + 1) % n], ring[i]) for i in range(n)]
    width = cols // (2 * pieces)
    parts = [local[:, j * width:(j + 1) * width] for j in range(2 * pieces)]
    full = jnp.zeros((n * rows, cols), local.dtype)
    for k in range(1, n):
        from_cw = tok_at(my_pos - k + n)
        from_ccw = tok_at(my_pos + k)
        for j in range(2 * pieces):
            clockwise = j % 2 == 0
            parts[j] = lax.ppermute(parts[j], axis, cw if clockwise else ccw)
            origin = from_cw if clockwise else from_ccw
            full = lax.dynamic_update_slice(full, parts[j], (origin * rows, j * width))
            if on_piece is not None:
                on_piece(origin, j, parts[j])
    full, local = lax.optimization_barrier((full, local))
    return lax.dynamic_update_slice(full, local, (me * rows, 0))


def tree_sum(v, axis):
    n = lax.axis_size(axis)
    if n & (n - 1):
        return lax.psum(v, axis)
    b = 1
    while b < n:
        v = v + lax.ppermute(v, axis, [(i, i ^ b) for i in range(n)])
        b *= 2
    return v


def packed_score(packed, count, size):
    gram = [[packed[m * count + k] for k in range(count)] for m in range(count)]
    member_obs = [packed[count * count + m] for m in range(count)]
    obs_sq = packed[count * count + count]
    diag = [gram[m][m] for m in range(count)]
    to_obs = [jnp.sqrt((diag[m] - 2.0 * member_obs[m] + obs_sq) / size + epsilon) for m in range(count)]
    pair = [[None] * count for _ in range(count)]
    pair_total = 0.0
    for m in range(count):
        for k in range(count):
            if m != k:
                pair[m][k] = jnp.sqrt((diag[m] + diag[k] - 2.0 * gram[m][k]) / size + epsilon)
                pair_total = pair_total + pair[m][k]
    energy = sum(to_obs) / count - pair_total / (2.0 * count * (count - 1))
    obs_coeff = [1.0 / (count * to_obs[m]) for m in range(count)]
    rows = []
    for m in range(count):
        row = []
        off = 0.0
        for k in range(count):
            if m != k:
                c = 1.0 / (count * (count - 1) * pair[m][k])
                off = off + c
                row.append(c)
            else:
                row.append(None)
        row[m] = obs_coeff[m] - off
        rows.append(jnp.stack(row))
    return (energy, jnp.stack(rows), -jnp.stack(obs_coeff))


def per_device(inputs, obs, weights, gains):
    sec = lax.axis_index("section")
    on_first = sec == 0
    gain = gains[0]
    tok_rows = obs.shape[0]
    width = obs.shape[1]
    size = float(tok_rows * lax.axis_size("tok") * width)

    obs_sq = jnp.einsum("rd,rd->", obs, obs, preferred_element_type=jnp.float32)

    members = inputs.shape[0]
    rows_all = inputs.reshape(members * tok_rows, width)
    n_tok = lax.axis_size("tok")
    local = weights[0]
    rows_w = local.shape[0]
    pieces = 2
    piece_w = width // (2 * pieces)
    overlap = RING_GATHER and n_tok % 2 == 0 and 2 < n_tok <= 16

    if overlap:
        acc = [None] * (2 * pieces)
        normed = []

        def on_piece(origin, j, piece):
            if not normed:
                rows_in, piece = lax.optimization_barrier((rows_all, piece))
                normed.append(norm_part(rows_in, gain))
            normed_a = normed[0][3]
            lhs = lax.dynamic_slice(normed_a, (0, origin * rows_w), (normed_a.shape[0], rows_w))
            term = jnp.dot(lhs, piece, preferred_element_type=jnp.float32)
            acc[j] = term if acc[j] is None else acc[j] + term

        weight = ring_gather(local, "tok", pieces, on_piece)
        values_a, unit_a, std_a, normed_a = normed[0]
        me = lax.axis_index("tok")
        lhs = lax.dynamic_slice(normed_a, (0, me * rows_w), (normed_a.shape[0], rows_w))
        for j in range(2 * pieces):
            acc[j] = acc[j] + jnp.dot(
                lhs, local[:, j * piece_w:(j + 1) * piece_w], preferred_element_type=jnp.float32
            )
        pre_a = jnp.concatenate(acc, axis=1)
        out_a = (values_a + gelu_value(pre_a)).astype(jnp.bfloat16)
        fa = (out_a, unit_a, std_a, pre_a)
    else:
        if RING_GATHER:
            weight = ring_gather(local, "tok")
        else:
            weight = lax.all_gather(weights, "tok", axis=1, tiled=True)[0]
        inputs, weight = lax.optimization_barrier((inputs, weight))
        rows_all = inputs.reshape(members * tok_rows, width)
        fa = section_forward(rows_all, gain, weight)
    arrived = shifted(fa[0], "section", 1)
    fb = section_forward(arrived, gain, weight)

    y = fb[0].reshape(members, tok_rows, width)
    obs_f = obs.astype(jnp.float32)
    yf = y.astype(jnp.float32)
    terms = []
    for m in range(members):
        for k in range(members):
            terms.append(jnp.sum(yf[m] * yf[k], axis=-1))
    for m in range(members):
        terms.append(jnp.sum(yf[m] * obs_f, axis=-1))
    terms = jnp.sum(jnp.stack(terms), axis=-1)
    packed = tree_sum(jnp.concatenate([terms, obs_sq.reshape(1)]), "tok")
    slope_a, slope_b = lax.optimization_barrier((gelu_slope(fa[3]), gelu_slope(fb[3])))
    member_gram = packed[: members * members].reshape(members, members)
    obs_rows = packed[members * members : members * members + members]
    obs_total = packed[members * members + members]
    energy, member_coeff, obs_coeff = score_terms(member_gram, obs_rows, obs_total, size)
    energy_arr = jnp.reshape(energy, (1,))

    cot = obs_coeff[:, None, None] * obs_f[None]
    for k in range(members):
        cot = cot + member_coeff[:, k, None, None] * y[k].astype(jnp.float32)[None]
    cot = cot.reshape(members * tok_rows, width)

    da = section_backward(cot, gain, weight, fb[1], fb[2], slope_b)
    back, energy_peer = shifted((da, energy_arr), "section", -1)
    energy_out = jnp.where(on_first, energy_peer, energy_arr)
    db = section_backward(back.astype(jnp.float32), gain, weight, fa[1], fa[2], slope_a)
    grads = jnp.where(on_first, db, da).reshape(members, tok_rows, width)
    return (grads[None], energy_out)


def solution(mesh):
    in_specs = (
        P("groups", "tok", None),
        P(("groups", "tok"), None),
        P("section", "tok", None),
        P("section", None),
    )
    out_specs = (P("section", "groups", "tok", None), P("groups"))
    return jax.shard_map(
        per_device, mesh=mesh, in_specs=in_specs, out_specs=out_specs, check_vma=False
    )
```

```python
import math

import jax
import jax.numpy as jnp
from jax import lax
from jax.sharding import PartitionSpec as P

epsilon = 1e-05
gelu_scale = math.sqrt(2.0 / math.pi)
cubic_term = 0.044715

RING_GATHER = True


def shifted(x, axis, by):
    size = lax.axis_size(axis)
    pairs = [(i, i + by) for i in range(size) if 0 <= i + by < size]
    return lax.ppermute(x, axis, pairs)


def gelu_value(pre_act):
    inner = jnp.tanh(gelu_scale * (pre_act + cubic_term * pre_act * pre_act * pre_act))
    return 0.5 * pre_act * (1.0 + inner)


def gelu_slope(pre_act):
    inner = jnp.tanh(gelu_scale * (pre_act + cubic_term * pre_act * pre_act * pre_act))
    return 0.5 * (1.0 + inner) + 0.5 * pre_act * (1.0 - inner * inner) * gelu_scale * (
        1.0 + 3.0 * cubic_term * pre_act * pre_act
    )


def norm_part(rows_in, gain):
    values = rows_in.astype(jnp.float32)
    row_mean = jnp.mean(values, axis=-1, keepdims=True)
    centred = values - row_mean
    inv_std = lax.rsqrt(jnp.mean(centred * centred, axis=-1, keepdims=True) + epsilon)
    unit_rows = centred * inv_std
    normed = (unit_rows * gain).astype(jnp.bfloat16)
    return (values, unit_rows, inv_std, normed)


def section_forward(rows_in, gain, weight):
    values = rows_in.astype(jnp.float32)
    row_mean = jnp.mean(values, axis=-1, keepdims=True)
    centred = values - row_mean
    inv_std = lax.rsqrt(jnp.mean(centred * centred, axis=-1, keepdims=True) + epsilon)
    unit_rows = centred * inv_std
    normed = (unit_rows * gain).astype(jnp.bfloat16)
    pre_act = jnp.dot(normed, weight, preferred_element_type=jnp.float32)
    output = (values + gelu_value(pre_act)).astype(jnp.bfloat16)
    return (output, unit_rows, inv_std, pre_act)


def section_backward(grad_out, gain, weight, unit_rows, inv_std, slope):
    grad_pre = (grad_out * slope).astype(jnp.bfloat16)
    grad_norm = lax.dot_general(
        grad_pre, weight, (((1,), (1,)), ((), ())), preferred_element_type=jnp.float32
    )
    scaled = grad_norm * gain
    grad_in = grad_out + inv_std * (
        scaled
        - jnp.mean(scaled, axis=-1, keepdims=True)
        - unit_rows * jnp.mean(scaled * unit_rows, axis=-1, keepdims=True)
    )
    return grad_in.astype(jnp.bfloat16)


def score_terms(member_gram, member_obs, obs_sq, size):
    count = member_gram.shape[0]
    diag_vals = jnp.diagonal(member_gram)
    apart = diag_vals[:, None] + diag_vals[None, :] - 2.0 * member_gram
    same = jnp.eye(count, dtype=jnp.float32)
    others = 1.0 - same
    pair_dist = jnp.sqrt(jnp.where(same > 0.5, size, apart) / size + epsilon)
    to_obs = jnp.sqrt((diag_vals - 2.0 * member_obs + obs_sq) / size + epsilon)
    energy = jnp.mean(to_obs) - jnp.sum(others * pair_dist) / (2.0 * count * (count - 1))
    pair_coeff = others / (count * (count - 1) * pair_dist)
    obs_coeff = 1.0 / (count * to_obs)
    member_coeff = pair_coeff + same * (obs_coeff - jnp.sum(pair_coeff, axis=1))[:, None]
    return (energy, member_coeff, -obs_coeff)


def snake_ring(n):
    if n % 2:
        return list(range(n))
    return list(range(0, n, 2)) + list(range(n - 1, 0, -2))


def ring_gather(local, axis, pieces=2, on_piece=None):
    n = lax.axis_size(axis)
    rows, cols = local.shape
    if n == 1 or n % 2:
        return lax.all_gather(local, axis, axis=0, tiled=True)
    ring = snake_ring(n)
    me = lax.axis_index(axis)
    my_pos = jnp.where(me % 2 == 0, me // 2, n - (me + 1) // 2)

    def tok_at(p):
        p = p % n
        return jnp.where(p < n // 2, 2 * p, 2 * (n - 1 - p) + 1)

    cw = [(ring[i], ring[(i + 1) % n]) for i in range(n)]
    ccw = [(ring[(i + 1) % n], ring[i]) for i in range(n)]
    width = cols // (2 * pieces)
    parts = [local[:, j * width:(j + 1) * width] for j in range(2 * pieces)]
    full = jnp.zeros((n * rows, cols), local.dtype)
    for k in range(1, n):
        from_cw = tok_at(my_pos - k + n)
        from_ccw = tok_at(my_pos + k)
        for j in range(2 * pieces):
            clockwise = j % 2 == 0
            parts[j] = lax.ppermute(parts[j], axis, cw if clockwise else ccw)
            origin = from_cw if clockwise else from_ccw
            full = lax.dynamic_update_slice(full, parts[j], (origin * rows, j * width))
            if on_piece is not None:
                on_piece(origin, j, parts[j])
    full, local = lax.optimization_barrier((full, local))
    return lax.dynamic_update_slice(full, local, (me * rows, 0))


def tree_sum(v, axis):
    n = lax.axis_size(axis)
    if n & (n - 1):
        return lax.psum(v, axis)
    b = 1
    while b < n:
        v = v + lax.ppermute(v, axis, [(i, i ^ b) for i in range(n)])
        b *= 2
    return v


def packed_score(packed, count, size):
    gram = [[packed[m * count + k] for k in range(count)] for m in range(count)]
    member_obs = [packed[count * count + m] for m in range(count)]
    obs_sq = packed[count * count + count]
    diag = [gram[m][m] for m in range(count)]
    to_obs = [jnp.sqrt((diag[m] - 2.0 * member_obs[m] + obs_sq) / size + epsilon) for m in range(count)]
    pair = [[None] * count for _ in range(count)]
    pair_total = 0.0
    for m in range(count):
        for k in range(count):
            if m != k:
                pair[m][k] = jnp.sqrt((diag[m] + diag[k] - 2.0 * gram[m][k]) / size + epsilon)
                pair_total = pair_total + pair[m][k]
    energy = sum(to_obs) / count - pair_total / (2.0 * count * (count - 1))
    obs_coeff = [1.0 / (count * to_obs[m]) for m in range(count)]
    rows = []
    for m in range(count):
        row = []
        off = 0.0
        for k in range(count):
            if m != k:
                c = 1.0 / (count * (count - 1) * pair[m][k])
                off = off + c
                row.append(c)
            else:
                row.append(None)
        row[m] = obs_coeff[m] - off
        rows.append(jnp.stack(row))
    return (energy, jnp.stack(rows), -jnp.stack(obs_coeff))


def per_device(inputs, obs, weights, gains):
    sec = lax.axis_index("section")
    on_first = sec == 0
    gain = gains[0]
    tok_rows = obs.shape[0]
    width = obs.shape[1]
    size = float(tok_rows * lax.axis_size("tok") * width)

    obs_sq = jnp.einsum("rd,rd->", obs, obs, preferred_element_type=jnp.float32)

    members = inputs.shape[0]
    rows_all = inputs.reshape(members * tok_rows, width)
    n_tok = lax.axis_size("tok")
    local = weights[0]
    rows_w = local.shape[0]
    pieces = 2
    piece_w = width // (2 * pieces)
    overlap = RING_GATHER and n_tok % 2 == 0 and 2 < n_tok <= 16

    if overlap:
        acc = [None] * (2 * pieces)
        normed = []

        def on_piece(origin, j, piece):
            if not normed:
                rows_in, piece = lax.optimization_barrier((rows_all, piece))
                normed.append(norm_part(rows_in, gain))
            normed_a = normed[0][3]
            lhs = lax.dynamic_slice(normed_a, (0, origin * rows_w), (normed_a.shape[0], rows_w))
            term = jnp.dot(lhs, piece, preferred_element_type=jnp.float32)
            acc[j] = term if acc[j] is None else acc[j] + term

        weight = ring_gather(local, "tok", pieces, on_piece)
        values_a, unit_a, std_a, normed_a = normed[0]
        me = lax.axis_index("tok")
        lhs = lax.dynamic_slice(normed_a, (0, me * rows_w), (normed_a.shape[0], rows_w))
        for j in range(2 * pieces):
            acc[j] = acc[j] + jnp.dot(
                lhs, local[:, j * piece_w:(j + 1) * piece_w], preferred_element_type=jnp.float32
            )
        pre_a = jnp.concatenate(acc, axis=1)
        out_a = (values_a + gelu_value(pre_a)).astype(jnp.bfloat16)
        fa = (out_a, unit_a, std_a, pre_a)
    else:
        if RING_GATHER:
            weight = ring_gather(local, "tok")
        else:
            weight = lax.all_gather(weights, "tok", axis=1, tiled=True)[0]
        inputs, weight = lax.optimization_barrier((inputs, weight))
        rows_all = inputs.reshape(members * tok_rows, width)
        fa = section_forward(rows_all, gain, weight)
    arrived = shifted(fa[0], "section", 1)
    fb = section_forward(arrived, gain, weight)

    y = fb[0].reshape(members, tok_rows, width)
    obs_f = obs.astype(jnp.float32)
    yf = y.astype(jnp.float32)
    terms = []
    for m in range(members):
        for k in range(members):
            terms.append(jnp.sum(yf[m] * yf[k], axis=-1))
    for m in range(members):
        terms.append(jnp.sum(yf[m] * obs_f, axis=-1))
    terms = jnp.sum(jnp.stack(terms), axis=-1)
    packed = tree_sum(jnp.concatenate([terms, obs_sq.reshape(1)]), "tok")
    slope_a, slope_b = lax.optimization_barrier((gelu_slope(fa[3]), gelu_slope(fb[3])))
    member_gram = packed[: members * members].reshape(members, members)
    obs_rows = packed[members * members : members * members + members]
    obs_total = packed[members * members + members]
    energy, member_coeff, obs_coeff = score_terms(member_gram, obs_rows, obs_total, size)
    energy_arr = jnp.reshape(energy, (1,))

    def second_backward():
        cot = obs_coeff[:, None, None] * obs_f[None]
        for k in range(members):
            cot = cot + member_coeff[:, k, None, None] * y[k].astype(jnp.float32)[None]
        cot = cot.reshape(members * tok_rows, width)
        return section_backward(cot, gain, weight, fb[1], fb[2], slope_b)

    da = lax.cond(on_first, lambda: jnp.zeros((members * tok_rows, width), jnp.bfloat16), second_backward)
    back, energy_peer = shifted((da, energy_arr), "section", -1)
    energy_out = jnp.where(on_first, energy_peer, energy_arr)
    grads = lax.cond(
        on_first,
        lambda: section_backward(back.astype(jnp.float32), gain, weight, fa[1], fa[2], slope_a),
        lambda: da,
    )
    grads = grads.reshape(members, tok_rows, width)
    return (grads[None], energy_out)


def solution(mesh):
    in_specs = (
        P("groups", "tok", None),
        P(("groups", "tok"), None),
        P("section", "tok", None),
        P("section", None),
    )
    out_specs = (P("section", "groups", "tok", None), P("groups"))
    return jax.shard_map(
        per_device, mesh=mesh, in_specs=in_specs, out_specs=out_specs, check_vma=False
    )
```

```python
import math

import jax
import jax.numpy as jnp
from jax import lax
from jax.sharding import PartitionSpec as P

epsilon = 1e-05
gelu_scale = math.sqrt(2.0 / math.pi)
cubic_term = 0.044715

RING_GATHER = True


def shifted(x, axis, by):
    size = lax.axis_size(axis)
    pairs = [(i, i + by) for i in range(size) if 0 <= i + by < size]
    return lax.ppermute(x, axis, pairs)


def gelu_value(pre_act):
    inner = jnp.tanh(gelu_scale * (pre_act + cubic_term * pre_act * pre_act * pre_act))
    return 0.5 * pre_act * (1.0 + inner)


def gelu_slope(pre_act):
    inner = jnp.tanh(gelu_scale * (pre_act + cubic_term * pre_act * pre_act * pre_act))
    return 0.5 * (1.0 + inner) + 0.5 * pre_act * (1.0 - inner * inner) * gelu_scale * (
        1.0 + 3.0 * cubic_term * pre_act * pre_act
    )


def norm_part(rows_in, gain):
    values = rows_in.astype(jnp.float32)
    row_mean = jnp.mean(values, axis=-1, keepdims=True)
    centred = values - row_mean
    inv_std = lax.rsqrt(jnp.mean(centred * centred, axis=-1, keepdims=True) + epsilon)
    unit_rows = centred * inv_std
    normed = (unit_rows * gain).astype(jnp.bfloat16)
    return (values, unit_rows, inv_std, normed)


def section_forward(rows_in, gain, weight):
    values = rows_in.astype(jnp.float32)
    row_mean = jnp.mean(values, axis=-1, keepdims=True)
    centred = values - row_mean
    inv_std = lax.rsqrt(jnp.mean(centred * centred, axis=-1, keepdims=True) + epsilon)
    unit_rows = centred * inv_std
    normed = (unit_rows * gain).astype(jnp.bfloat16)
    pre_act = jnp.dot(normed, weight, preferred_element_type=jnp.float32)
    output = (values + gelu_value(pre_act)).astype(jnp.bfloat16)
    return (output, unit_rows, inv_std, pre_act)


def section_backward(grad_out, gain, weight, unit_rows, inv_std, slope):
    grad_pre = (grad_out * slope).astype(jnp.bfloat16)
    grad_norm = lax.dot_general(
        grad_pre, weight, (((1,), (1,)), ((), ())), preferred_element_type=jnp.float32
    )
    scaled = grad_norm * gain
    grad_in = grad_out + inv_std * (
        scaled
        - jnp.mean(scaled, axis=-1, keepdims=True)
        - unit_rows * jnp.mean(scaled * unit_rows, axis=-1, keepdims=True)
    )
    return grad_in.astype(jnp.bfloat16)


def score_terms(member_gram, member_obs, obs_sq, size):
    count = member_gram.shape[0]
    diag_vals = jnp.diagonal(member_gram)
    apart = diag_vals[:, None] + diag_vals[None, :] - 2.0 * member_gram
    same = jnp.eye(count, dtype=jnp.float32)
    others = 1.0 - same
    pair_dist = jnp.sqrt(jnp.where(same > 0.5, size, apart) / size + epsilon)
    to_obs = jnp.sqrt((diag_vals - 2.0 * member_obs + obs_sq) / size + epsilon)
    energy = jnp.mean(to_obs) - jnp.sum(others * pair_dist) / (2.0 * count * (count - 1))
    pair_coeff = others / (count * (count - 1) * pair_dist)
    obs_coeff = 1.0 / (count * to_obs)
    member_coeff = pair_coeff + same * (obs_coeff - jnp.sum(pair_coeff, axis=1))[:, None]
    return (energy, member_coeff, -obs_coeff)


def snake_ring(n):
    if n % 2:
        return list(range(n))
    return list(range(0, n, 2)) + list(range(n - 1, 0, -2))


def ring_gather(local, axis, pieces=2, on_piece=None):
    n = lax.axis_size(axis)
    rows, cols = local.shape
    if n == 1 or n % 2:
        return lax.all_gather(local, axis, axis=0, tiled=True)
    ring = snake_ring(n)
    me = lax.axis_index(axis)
    my_pos = jnp.where(me % 2 == 0, me // 2, n - (me + 1) // 2)

    def tok_at(p):
        p = p % n
        return jnp.where(p < n // 2, 2 * p, 2 * (n - 1 - p) + 1)

    cw = [(ring[i], ring[(i + 1) % n]) for i in range(n)]
    ccw = [(ring[(i + 1) % n], ring[i]) for i in range(n)]
    width = cols // (2 * pieces)
    parts = [local[:, j * width:(j + 1) * width] for j in range(2 * pieces)]
    full = jnp.zeros((n * rows, cols), local.dtype)
    for k in range(1, n):
        from_cw = tok_at(my_pos - k + n)
        from_ccw = tok_at(my_pos + k)
        for j in range(2 * pieces):
            clockwise = j % 2 == 0
            parts[j] = lax.ppermute(parts[j], axis, cw if clockwise else ccw)
            origin = from_cw if clockwise else from_ccw
            full = lax.dynamic_update_slice(full, parts[j], (origin * rows, j * width))
            if on_piece is not None:
                on_piece(origin, j, parts[j])
    full, local = lax.optimization_barrier((full, local))
    return lax.dynamic_update_slice(full, local, (me * rows, 0))


def tree_sum(v, axis):
    n = lax.axis_size(axis)
    if n & (n - 1):
        return lax.psum(v, axis)
    b = 1
    while b < n:
        v = v + lax.ppermute(v, axis, [(i, i ^ b) for i in range(n)])
        b *= 2
    return v


def packed_score(packed, count, size):
    gram = [[packed[m * count + k] for k in range(count)] for m in range(count)]
    member_obs = [packed[count * count + m] for m in range(count)]
    obs_sq = packed[count * count + count]
    diag = [gram[m][m] for m in range(count)]
    to_obs = [jnp.sqrt((diag[m] - 2.0 * member_obs[m] + obs_sq) / size + epsilon) for m in range(count)]
    pair = [[None] * count for _ in range(count)]
    pair_total = 0.0
    for m in range(count):
        for k in range(count):
            if m != k:
                pair[m][k] = jnp.sqrt((diag[m] + diag[k] - 2.0 * gram[m][k]) / size + epsilon)
                pair_total = pair_total + pair[m][k]
    energy = sum(to_obs) / count - pair_total / (2.0 * count * (count - 1))
    obs_coeff = [1.0 / (count * to_obs[m]) for m in range(count)]
    rows = []
    for m in range(count):
        row = []
        off = 0.0
        for k in range(count):
            if m != k:
                c = 1.0 / (count * (count - 1) * pair[m][k])
                off = off + c
                row.append(c)
            else:
                row.append(None)
        row[m] = obs_coeff[m] - off
        rows.append(jnp.stack(row))
    return (energy, jnp.stack(rows), -jnp.stack(obs_coeff))


def per_device(inputs, obs, weights, gains):
    sec = lax.axis_index("section")
    on_first = sec == 0
    gain = gains[0]
    tok_rows = obs.shape[0]
    width = obs.shape[1]
    size = float(tok_rows * lax.axis_size("tok") * width)

    obs_sq = jnp.einsum("rd,rd->", obs, obs, preferred_element_type=jnp.float32)

    members = inputs.shape[0]
    rows_all = inputs.reshape(members * tok_rows, width)
    n_tok = lax.axis_size("tok")
    local = weights[0]
    rows_w = local.shape[0]
    pieces = 2
    piece_w = width // (2 * pieces)
    overlap = RING_GATHER and n_tok % 2 == 0 and 2 < n_tok <= 16

    if overlap:
        acc = [None] * (2 * pieces)
        normed = []

        def on_piece(origin, j, piece):
            if not normed:
                rows_in, piece = lax.optimization_barrier((rows_all, piece))
                normed.append(norm_part(rows_in, gain))
            normed_a = normed[0][3]
            lhs = lax.dynamic_slice(normed_a, (0, origin * rows_w), (normed_a.shape[0], rows_w))
            term = jnp.dot(lhs, piece, preferred_element_type=jnp.float32)
            acc[j] = term if acc[j] is None else acc[j] + term

        weight = ring_gather(local, "tok", pieces, on_piece)
        values_a, unit_a, std_a, normed_a = normed[0]
        me = lax.axis_index("tok")
        lhs = lax.dynamic_slice(normed_a, (0, me * rows_w), (normed_a.shape[0], rows_w))
        for j in range(2 * pieces):
            acc[j] = acc[j] + jnp.dot(
                lhs, local[:, j * piece_w:(j + 1) * piece_w], preferred_element_type=jnp.float32
            )
        pre_a = jnp.concatenate(acc, axis=1)
        out_a = (values_a + gelu_value(pre_a)).astype(jnp.bfloat16)
        fa = (out_a, unit_a, std_a, pre_a)
    else:
        if RING_GATHER:
            weight = ring_gather(local, "tok")
        else:
            weight = lax.all_gather(weights, "tok", axis=1, tiled=True)[0]
        inputs, weight = lax.optimization_barrier((inputs, weight))
        rows_all = inputs.reshape(members * tok_rows, width)
        fa = section_forward(rows_all, gain, weight)
    arrived = shifted(fa[0], "section", 1)
    fb = section_forward(arrived, gain, weight)

    y = fb[0].reshape(members, tok_rows, width)
    obs_f = obs.astype(jnp.float32)
    yf = y.astype(jnp.float32)
    terms = []
    for m in range(members):
        for k in range(members):
            terms.append(jnp.sum(yf[m] * yf[k], axis=-1))
    for m in range(members):
        terms.append(jnp.sum(yf[m] * obs_f, axis=-1))
    terms = jnp.sum(jnp.stack(terms), axis=-1)
    packed = jnp.sum(lax.all_gather(jnp.concatenate([terms, obs_sq.reshape(1)]), "tok"), axis=0)
    slope_a, slope_b = lax.optimization_barrier((gelu_slope(fa[3]), gelu_slope(fb[3])))
    member_gram = packed[: members * members].reshape(members, members)
    obs_rows = packed[members * members : members * members + members]
    obs_total = packed[members * members + members]
    energy, member_coeff, obs_coeff = score_terms(member_gram, obs_rows, obs_total, size)
    energy_arr = jnp.reshape(energy, (1,))

    def second_backward():
        cot = obs_coeff[:, None, None] * obs_f[None]
        for k in range(members):
            cot = cot + member_coeff[:, k, None, None] * y[k].astype(jnp.float32)[None]
        cot = cot.reshape(members * tok_rows, width)
        return section_backward(cot, gain, weight, fb[1], fb[2], slope_b)

    da = lax.cond(on_first, lambda: jnp.zeros((members * tok_rows, width), jnp.bfloat16), second_backward)
    back, energy_peer = shifted((da, energy_arr), "section", -1)
    energy_out = jnp.where(on_first, energy_peer, energy_arr)
    grads = lax.cond(
        on_first,
        lambda: section_backward(back.astype(jnp.float32), gain, weight, fa[1], fa[2], slope_a),
        lambda: da,
    )
    grads = grads.reshape(members, tok_rows, width)
    return (grads[None], energy_out)


def solution(mesh):
    in_specs = (
        P("groups", "tok", None),
        P(("groups", "tok"), None),
        P("section", "tok", None),
        P("section", None),
    )
    out_specs = (P("section", "groups", "tok", None), P("groups"))
    return jax.shard_map(
        per_device, mesh=mesh, in_specs=in_specs, out_specs=out_specs, check_vma=False
    )
```

```python
import math

import jax
import jax.numpy as jnp
from jax import lax
from jax.sharding import PartitionSpec as P

epsilon = 1e-05
gelu_scale = math.sqrt(2.0 / math.pi)
cubic_term = 0.044715

RING_GATHER = True


def shifted(x, axis, by):
    size = lax.axis_size(axis)
    pairs = [(i, i + by) for i in range(size) if 0 <= i + by < size]
    return lax.ppermute(x, axis, pairs)


def gelu_value(pre_act):
    inner = jnp.tanh(gelu_scale * (pre_act + cubic_term * pre_act * pre_act * pre_act))
    return 0.5 * pre_act * (1.0 + inner)


def gelu_slope(pre_act):
    inner = jnp.tanh(gelu_scale * (pre_act + cubic_term * pre_act * pre_act * pre_act))
    return 0.5 * (1.0 + inner) + 0.5 * pre_act * (1.0 - inner * inner) * gelu_scale * (
        1.0 + 3.0 * cubic_term * pre_act * pre_act
    )


def norm_part(rows_in, gain):
    values = rows_in.astype(jnp.float32)
    row_mean = jnp.mean(values, axis=-1, keepdims=True)
    centred = values - row_mean
    inv_std = lax.rsqrt(jnp.mean(centred * centred, axis=-1, keepdims=True) + epsilon)
    unit_rows = centred * inv_std
    normed = (unit_rows * gain).astype(jnp.bfloat16)
    return (values, unit_rows, inv_std, normed)


def section_forward(rows_in, gain, weight):
    values = rows_in.astype(jnp.float32)
    row_mean = jnp.mean(values, axis=-1, keepdims=True)
    centred = values - row_mean
    inv_std = lax.rsqrt(jnp.mean(centred * centred, axis=-1, keepdims=True) + epsilon)
    unit_rows = centred * inv_std
    normed = (unit_rows * gain).astype(jnp.bfloat16)
    pre_act = jnp.dot(normed, weight, preferred_element_type=jnp.float32)
    output = (values + gelu_value(pre_act)).astype(jnp.bfloat16)
    return (output, unit_rows, inv_std, pre_act)


def section_backward(grad_out, gain, weight, unit_rows, inv_std, slope):
    grad_pre = (grad_out * slope).astype(jnp.bfloat16)
    grad_norm = lax.dot_general(
        grad_pre, weight, (((1,), (1,)), ((), ())), preferred_element_type=jnp.float32
    )
    scaled = grad_norm * gain
    grad_in = grad_out + inv_std * (
        scaled
        - jnp.mean(scaled, axis=-1, keepdims=True)
        - unit_rows * jnp.mean(scaled * unit_rows, axis=-1, keepdims=True)
    )
    return grad_in.astype(jnp.bfloat16)


def score_terms(member_gram, member_obs, obs_sq, size):
    count = member_gram.shape[0]
    diag_vals = jnp.diagonal(member_gram)
    apart = diag_vals[:, None] + diag_vals[None, :] - 2.0 * member_gram
    same = jnp.eye(count, dtype=jnp.float32)
    others = 1.0 - same
    pair_dist = jnp.sqrt(jnp.where(same > 0.5, size, apart) / size + epsilon)
    to_obs = jnp.sqrt((diag_vals - 2.0 * member_obs + obs_sq) / size + epsilon)
    energy = jnp.mean(to_obs) - jnp.sum(others * pair_dist) / (2.0 * count * (count - 1))
    pair_coeff = others / (count * (count - 1) * pair_dist)
    obs_coeff = 1.0 / (count * to_obs)
    member_coeff = pair_coeff + same * (obs_coeff - jnp.sum(pair_coeff, axis=1))[:, None]
    return (energy, member_coeff, -obs_coeff)


def snake_ring(n):
    if n % 2:
        return list(range(n))
    return list(range(0, n, 2)) + list(range(n - 1, 0, -2))


def ring_gather(local, axis, pieces=2, on_piece=None):
    n = lax.axis_size(axis)
    rows, cols = local.shape
    if n == 1 or n % 2:
        return lax.all_gather(local, axis, axis=0, tiled=True)
    ring = snake_ring(n)
    me = lax.axis_index(axis)
    my_pos = jnp.where(me % 2 == 0, me // 2, n - (me + 1) // 2)

    def tok_at(p):
        p = p % n
        return jnp.where(p < n // 2, 2 * p, 2 * (n - 1 - p) + 1)

    cw = [(ring[i], ring[(i + 1) % n]) for i in range(n)]
    ccw = [(ring[(i + 1) % n], ring[i]) for i in range(n)]
    width = cols // (2 * pieces)
    parts = [local[:, j * width:(j + 1) * width] for j in range(2 * pieces)]
    full = jnp.zeros((n * rows, cols), local.dtype)
    for k in range(1, n):
        from_cw = tok_at(my_pos - k + n)
        from_ccw = tok_at(my_pos + k)
        for j in range(2 * pieces):
            clockwise = j % 2 == 0
            parts[j] = lax.ppermute(parts[j], axis, cw if clockwise else ccw)
            origin = from_cw if clockwise else from_ccw
            full = lax.dynamic_update_slice(full, parts[j], (origin * rows, j * width))
            if on_piece is not None:
                on_piece(origin, j, parts[j])
    full, local = lax.optimization_barrier((full, local))
    return lax.dynamic_update_slice(full, local, (me * rows, 0))


def tree_sum(v, axis):
    n = lax.axis_size(axis)
    if n & (n - 1):
        return lax.psum(v, axis)
    b = 1
    while b < n:
        v = v + lax.ppermute(v, axis, [(i, i ^ b) for i in range(n)])
        b *= 2
    return v


def packed_score(packed, count, size):
    gram = [[packed[m * count + k] for k in range(count)] for m in range(count)]
    member_obs = [packed[count * count + m] for m in range(count)]
    obs_sq = packed[count * count + count]
    diag = [gram[m][m] for m in range(count)]
    to_obs = [jnp.sqrt((diag[m] - 2.0 * member_obs[m] + obs_sq) / size + epsilon) for m in range(count)]
    pair = [[None] * count for _ in range(count)]
    pair_total = 0.0
    for m in range(count):
        for k in range(count):
            if m != k:
                pair[m][k] = jnp.sqrt((diag[m] + diag[k] - 2.0 * gram[m][k]) / size + epsilon)
                pair_total = pair_total + pair[m][k]
    energy = sum(to_obs) / count - pair_total / (2.0 * count * (count - 1))
    obs_coeff = [1.0 / (count * to_obs[m]) for m in range(count)]
    rows = []
    for m in range(count):
        row = []
        off = 0.0
        for k in range(count):
            if m != k:
                c = 1.0 / (count * (count - 1) * pair[m][k])
                off = off + c
                row.append(c)
            else:
                row.append(None)
        row[m] = obs_coeff[m] - off
        rows.append(jnp.stack(row))
    return (energy, jnp.stack(rows), -jnp.stack(obs_coeff))


def per_device(inputs, obs, weights, gains):
    sec = lax.axis_index("section")
    on_first = sec == 0
    gain = gains[0]
    tok_rows = obs.shape[0]
    width = obs.shape[1]
    size = float(tok_rows * lax.axis_size("tok") * width)

    obs_sq = jnp.einsum("rd,rd->", obs, obs, preferred_element_type=jnp.float32)

    members = inputs.shape[0]
    rows_all = inputs.reshape(members * tok_rows, width)
    n_tok = lax.axis_size("tok")
    local = weights[0]
    rows_w = local.shape[0]
    pieces = 2
    piece_w = width // (2 * pieces)
    overlap = RING_GATHER and n_tok % 2 == 0 and 2 < n_tok <= 16

    if overlap:
        acc = [None] * (2 * pieces)
        normed = []

        def on_piece(origin, j, piece):
            if not normed:
                rows_in, piece = lax.optimization_barrier((rows_all, piece))
                normed.append(norm_part(rows_in, gain))
            normed_a = normed[0][3]
            lhs = lax.dynamic_slice(normed_a, (0, origin * rows_w), (normed_a.shape[0], rows_w))
            term = jnp.dot(lhs, piece, preferred_element_type=jnp.float32)
            acc[j] = term if acc[j] is None else acc[j] + term

        weight = ring_gather(local, "tok", pieces, on_piece)
        values_a, unit_a, std_a, normed_a = normed[0]
        me = lax.axis_index("tok")
        lhs = lax.dynamic_slice(normed_a, (0, me * rows_w), (normed_a.shape[0], rows_w))
        for j in range(2 * pieces):
            acc[j] = acc[j] + jnp.dot(
                lhs, local[:, j * piece_w:(j + 1) * piece_w], preferred_element_type=jnp.float32
            )
        pre_a = jnp.concatenate(acc, axis=1)
        out_a = (values_a + gelu_value(pre_a)).astype(jnp.bfloat16)
        fa = (out_a, unit_a, std_a, pre_a)
    else:
        if RING_GATHER:
            weight = ring_gather(local, "tok")
        else:
            weight = lax.all_gather(weights, "tok", axis=1, tiled=True)[0]
        inputs, weight = lax.optimization_barrier((inputs, weight))
        rows_all = inputs.reshape(members * tok_rows, width)
        fa = section_forward(rows_all, gain, weight)
    arrived = shifted(fa[0], "section", 1)
    fb = section_forward(arrived, gain, weight)

    y = fb[0].reshape(members, tok_rows, width)
    obs_f = obs.astype(jnp.float32)
    yf = y.astype(jnp.float32)
    terms = []
    for m in range(members):
        for k in range(members):
            terms.append(jnp.sum(yf[m] * yf[k], axis=-1))
    for m in range(members):
        terms.append(jnp.sum(yf[m] * obs_f, axis=-1))
    terms = jnp.sum(jnp.stack(terms), axis=-1)
    packed = tree_sum(jnp.concatenate([terms, obs_sq.reshape(1)]), "tok")
    slope_a, slope_b = lax.optimization_barrier((gelu_slope(fa[3]), gelu_slope(fb[3])))
    member_gram = packed[: members * members].reshape(members, members)
    obs_rows = packed[members * members : members * members + members]
    obs_total = packed[members * members + members]
    energy, member_coeff, obs_coeff = score_terms(member_gram, obs_rows, obs_total, size)
    energy_arr = jnp.reshape(energy, (1,))

    def second_backward():
        cot = obs_coeff[:, None, None] * obs_f[None]
        for k in range(members):
            cot = cot + member_coeff[:, k, None, None] * yf[k][None]
        cot = cot.reshape(members * tok_rows, width)
        return section_backward(cot, gain, weight, fb[1], fb[2], slope_b)

    da = lax.cond(on_first, lambda: jnp.zeros((members * tok_rows, width), jnp.bfloat16), second_backward)
    back, energy_peer = shifted((da, energy_arr), "section", -1)
    energy_out = jnp.where(on_first, energy_peer, energy_arr)
    grads = lax.cond(
        on_first,
        lambda: section_backward(back.astype(jnp.float32), gain, weight, fa[1], fa[2], slope_a),
        lambda: da,
    )
    grads = grads.reshape(members, tok_rows, width)
    return (grads[None], energy_out)


def solution(mesh):
    in_specs = (
        P("groups", "tok", None),
        P(("groups", "tok"), None),
        P("section", "tok", None),
        P("section", None),
    )
    out_specs = (P("section", "groups", "tok", None), P("groups"))
    return jax.shard_map(
        per_device, mesh=mesh, in_specs=in_specs, out_specs=out_specs, check_vma=False
    )
```

```python
import math

import jax
import jax.numpy as jnp
from jax import lax
from jax.sharding import PartitionSpec as P


epsilon = 1e-05
gelu_scale = math.sqrt(2.0 / math.pi)
cubic_term = 0.044715

RING_GATHER = True


def shifted(x, axis, by):
    size = lax.axis_size(axis)
    pairs = [(i, i + by) for i in range(size) if 0 <= i + by < size]
    return lax.ppermute(x, axis, pairs)


def gelu_value(pre_act):
    inner = jnp.tanh(gelu_scale * (pre_act + cubic_term * pre_act * pre_act * pre_act))
    return 0.5 * pre_act * (1.0 + inner)


def gelu_slope(pre_act):
    inner = jnp.tanh(gelu_scale * (pre_act + cubic_term * pre_act * pre_act * pre_act))
    return 0.5 * (1.0 + inner) + 0.5 * pre_act * (1.0 - inner * inner) * gelu_scale * (
        1.0 + 3.0 * cubic_term * pre_act * pre_act
    )


def norm_part(rows_in, gain):
    values = rows_in.astype(jnp.float32)
    row_mean = jnp.mean(values, axis=-1, keepdims=True)
    centred = values - row_mean
    inv_std = lax.rsqrt(jnp.mean(centred * centred, axis=-1, keepdims=True) + epsilon)
    unit_rows = centred * inv_std
    normed = (unit_rows * gain).astype(jnp.bfloat16)
    return (values, unit_rows, inv_std, normed)


def section_forward(rows_in, gain, weight):
    values = rows_in.astype(jnp.float32)
    row_mean = jnp.mean(values, axis=-1, keepdims=True)
    centred = values - row_mean
    inv_std = lax.rsqrt(jnp.mean(centred * centred, axis=-1, keepdims=True) + epsilon)
    unit_rows = centred * inv_std
    normed = (unit_rows * gain).astype(jnp.bfloat16)
    pre_act = jnp.dot(normed, weight, preferred_element_type=jnp.float32)
    output = (values + gelu_value(pre_act)).astype(jnp.bfloat16)
    return (output, unit_rows, inv_std, pre_act)


def section_backward(grad_out, gain, weight, unit_rows, inv_std, slope):
    grad_pre = (grad_out * slope).astype(jnp.bfloat16)
    grad_norm = lax.dot_general(
        grad_pre, weight, (((1,), (1,)), ((), ())), preferred_element_type=jnp.float32
    )
    scaled = grad_norm * gain
    grad_in = grad_out + inv_std * (
        scaled
        - jnp.mean(scaled, axis=-1, keepdims=True)
        - unit_rows * jnp.mean(scaled * unit_rows, axis=-1, keepdims=True)
    )
    return grad_in.astype(jnp.bfloat16)


def score_terms(member_gram, member_obs, obs_sq, size):
    count = member_gram.shape[0]
    diag_vals = jnp.diagonal(member_gram)
    apart = diag_vals[:, None] + diag_vals[None, :] - 2.0 * member_gram
    same = jnp.eye(count, dtype=jnp.float32)
    others = 1.0 - same
    pair_dist = jnp.sqrt(jnp.where(same > 0.5, size, apart) / size + epsilon)
    to_obs = jnp.sqrt((diag_vals - 2.0 * member_obs + obs_sq) / size + epsilon)
    energy = jnp.mean(to_obs) - jnp.sum(others * pair_dist) / (2.0 * count * (count - 1))
    pair_coeff = others / (count * (count - 1) * pair_dist)
    obs_coeff = 1.0 / (count * to_obs)
    member_coeff = pair_coeff + same * (obs_coeff - jnp.sum(pair_coeff, axis=1))[:, None]
    return (energy, member_coeff, -obs_coeff)


def snake_ring(n):
    if n % 2:
        return list(range(n))
    return list(range(0, n, 2)) + list(range(n - 1, 0, -2))


def ring_gather(local, axis, pieces=2, on_piece=None):
    n = lax.axis_size(axis)
    rows, cols = local.shape
    if n == 1 or n % 2:
        return lax.all_gather(local, axis, axis=0, tiled=True)
    ring = snake_ring(n)
    me = lax.axis_index(axis)
    my_pos = jnp.where(me % 2 == 0, me // 2, n - (me + 1) // 2)

    def tok_at(p):
        p = p % n
        return jnp.where(p < n // 2, 2 * p, 2 * (n - 1 - p) + 1)

    cw = [(ring[i], ring[(i + 1) % n]) for i in range(n)]
    ccw = [(ring[(i + 1) % n], ring[i]) for i in range(n)]
    width = cols // (2 * pieces)
    parts = [local[:, j * width:(j + 1) * width] for j in range(2 * pieces)]
    full = jnp.zeros((n * rows, cols), local.dtype)
    for k in range(1, n):
        from_cw = tok_at(my_pos - k + n)
        from_ccw = tok_at(my_pos + k)
        for j in range(2 * pieces):
            clockwise = j % 2 == 0
            parts[j] = lax.ppermute(parts[j], axis, cw if clockwise else ccw)
            origin = from_cw if clockwise else from_ccw
            full = lax.dynamic_update_slice(full, parts[j], (origin * rows, j * width))
            if on_piece is not None:
                on_piece(origin, j, parts[j])
    full, local = lax.optimization_barrier((full, local))
    return lax.dynamic_update_slice(full, local, (me * rows, 0))


def tree_sum(v, axis):
    n = lax.axis_size(axis)
    if n & (n - 1):
        return lax.psum(v, axis)
    b = 1
    while b < n:
        v = v + lax.ppermute(v, axis, [(i, i ^ b) for i in range(n)])
        b *= 2
    return v


def device_body(inputs, obs, weights, gains):
    sec = lax.axis_index("section")
    on_first = sec == 0
    gain = gains[0]
    tok_rows = obs.shape[0]
    width = obs.shape[1]
    size = float(tok_rows * lax.axis_size("tok") * width)

    obs_sq = jnp.einsum("rd,rd->", obs, obs, preferred_element_type=jnp.float32)

    members = inputs.shape[0]
    rows_all = inputs.reshape(members * tok_rows, width)
    n_tok = lax.axis_size("tok")
    local = weights[0]
    rows_w = local.shape[0]
    pieces = 2
    piece_w = width // (2 * pieces)
    overlap = RING_GATHER and n_tok % 2 == 0 and 2 < n_tok <= 16

    if overlap:
        acc = [None] * (2 * pieces)
        me = lax.axis_index("tok")
        values_a, unit_a, std_a, normed_a = norm_part(rows_all, gain)
        lhs = lax.dynamic_slice(normed_a, (0, me * rows_w), (normed_a.shape[0], rows_w))
        for j in range(2 * pieces):
            acc[j] = jnp.dot(
                lhs, local[:, j * piece_w:(j + 1) * piece_w], preferred_element_type=jnp.float32
            )

        def on_piece(origin, j, piece):
            lhs = lax.dynamic_slice(normed_a, (0, origin * rows_w), (normed_a.shape[0], rows_w))
            term = jnp.dot(lhs, piece, preferred_element_type=jnp.float32)
            acc[j] = term if acc[j] is None else acc[j] + term

        weight = ring_gather(local, "tok", pieces, on_piece)
        pre_a = jnp.concatenate(acc, axis=1)
        out_a = (values_a + gelu_value(pre_a)).astype(jnp.bfloat16)
        fa = (out_a, unit_a, std_a, pre_a)
    else:
        if RING_GATHER:
            weight = ring_gather(local, "tok")
        else:
            weight = lax.all_gather(weights, "tok", axis=1, tiled=True)[0]
        inputs, weight = lax.optimization_barrier((inputs, weight))
        rows_all = inputs.reshape(members * tok_rows, width)
        fa = section_forward(rows_all, gain, weight)
    arrived = shifted(fa[0], "section", 1)
    fb = section_forward(arrived, gain, weight)

    y = fb[0].reshape(members, tok_rows, width)
    obs_f = obs.astype(jnp.float32)
    yf = y.astype(jnp.float32)
    terms = []
    for m in range(members):
        for k in range(members):
            terms.append(jnp.sum(yf[m] * yf[k], axis=-1))
    for m in range(members):
        terms.append(jnp.sum(yf[m] * obs_f, axis=-1))
    terms = jnp.sum(jnp.stack(terms), axis=-1)
    packed = tree_sum(jnp.concatenate([terms, obs_sq.reshape(1)]), "tok")
    slope_a, slope_b = lax.optimization_barrier((gelu_slope(fa[3]), gelu_slope(fb[3])))
    member_gram = packed[: members * members].reshape(members, members)
    obs_rows = packed[members * members : members * members + members]
    obs_total = packed[members * members + members]
    energy, member_coeff, obs_coeff = score_terms(member_gram, obs_rows, obs_total, size)
    energy_arr = jnp.reshape(energy, (1,))

    def second_backward():
        cot = obs_coeff[:, None, None] * obs_f[None]
        for k in range(members):
            cot = cot + member_coeff[:, k, None, None] * y[k].astype(jnp.float32)[None]
        cot = cot.reshape(members * tok_rows, width)
        return section_backward(cot, gain, weight, fb[1], fb[2], slope_b)

    da = lax.cond(on_first, lambda: jnp.zeros((members * tok_rows, width), jnp.bfloat16), second_backward)
    back, energy_peer = shifted((da, energy_arr), "section", -1)
    energy_out = jnp.where(on_first, energy_peer, energy_arr)
    grads = lax.cond(
        on_first,
        lambda: section_backward(back.astype(jnp.float32), gain, weight, fa[1], fa[2], slope_a),
        lambda: da,
    )
    grads = grads.reshape(members, tok_rows, width)
    return (grads[None], energy_out)


def solution(mesh):
    in_specs = (
        P("groups", "tok", None),
        P(("groups", "tok"), None),
        P("section", "tok", None),
        P("section", None),
    )
    out_specs = (P("section", "groups", "tok", None), P("groups"))
    return jax.shard_map(
        device_body, mesh=mesh, in_specs=in_specs, out_specs=out_specs, check_vma=False
    )
```

```python
import math

import jax
import jax.numpy as jnp
from jax import lax
from jax.sharding import PartitionSpec as P

epsilon = 1e-05
gelu_scale = math.sqrt(2.0 / math.pi)
cubic_term = 0.044715

RING_GATHER = True


def shifted(x, axis, by):
    size = lax.axis_size(axis)
    pairs = [(i, i + by) for i in range(size) if 0 <= i + by < size]
    return lax.ppermute(x, axis, pairs)


def gelu_value(pre_act):
    inner = jnp.tanh(gelu_scale * (pre_act + cubic_term * pre_act * pre_act * pre_act))
    return 0.5 * pre_act * (1.0 + inner)


def gelu_slope(pre_act):
    inner = jnp.tanh(gelu_scale * (pre_act + cubic_term * pre_act * pre_act * pre_act))
    return 0.5 * (1.0 + inner) + 0.5 * pre_act * (1.0 - inner * inner) * gelu_scale * (
        1.0 + 3.0 * cubic_term * pre_act * pre_act
    )


def norm_part(rows_in, gain):
    values = rows_in.astype(jnp.float32)
    row_mean = jnp.mean(values, axis=-1, keepdims=True)
    centred = values - row_mean
    inv_std = lax.rsqrt(jnp.mean(centred * centred, axis=-1, keepdims=True) + epsilon)
    unit_rows = centred * inv_std
    normed = (unit_rows * gain).astype(jnp.bfloat16)
    return (values, unit_rows, inv_std, normed)


def section_forward(rows_in, gain, weight):
    values = rows_in.astype(jnp.float32)
    row_mean = jnp.mean(values, axis=-1, keepdims=True)
    centred = values - row_mean
    inv_std = lax.rsqrt(jnp.mean(centred * centred, axis=-1, keepdims=True) + epsilon)
    unit_rows = centred * inv_std
    normed = (unit_rows * gain).astype(jnp.bfloat16)
    pre_act = jnp.dot(normed, weight, preferred_element_type=jnp.float32)
    output = (values + gelu_value(pre_act)).astype(jnp.bfloat16)
    return (output, unit_rows, inv_std, pre_act)


def section_backward(grad_out, gain, weight, unit_rows, inv_std, slope):
    grad_pre = (grad_out * slope).astype(jnp.bfloat16)
    grad_norm = lax.dot_general(
        grad_pre, weight, (((1,), (1,)), ((), ())), preferred_element_type=jnp.float32
    )
    scaled = grad_norm * gain
    grad_in = grad_out + inv_std * (
        scaled
        - jnp.mean(scaled, axis=-1, keepdims=True)
        - unit_rows * jnp.mean(scaled * unit_rows, axis=-1, keepdims=True)
    )
    return grad_in.astype(jnp.bfloat16)


def score_terms(member_gram, member_obs, obs_sq, size):
    count = member_gram.shape[0]
    diag_vals = jnp.diagonal(member_gram)
    apart = diag_vals[:, None] + diag_vals[None, :] - 2.0 * member_gram
    same = jnp.eye(count, dtype=jnp.float32)
    others = 1.0 - same
    pair_dist = jnp.sqrt(jnp.where(same > 0.5, size, apart) / size + epsilon)
    to_obs = jnp.sqrt((diag_vals - 2.0 * member_obs + obs_sq) / size + epsilon)
    energy = jnp.mean(to_obs) - jnp.sum(others * pair_dist) / (2.0 * count * (count - 1))
    pair_coeff = others / (count * (count - 1) * pair_dist)
    obs_coeff = 1.0 / (count * to_obs)
    member_coeff = pair_coeff + same * (obs_coeff - jnp.sum(pair_coeff, axis=1))[:, None]
    return (energy, member_coeff, -obs_coeff)


def snake_ring(n):
    if n % 2:
        return list(range(n))
    return list(range(0, n, 2)) + list(range(n - 1, 0, -2))


def ring_gather(local, axis, pieces=2, on_piece=None):
    n = lax.axis_size(axis)
    rows, cols = local.shape
    if n == 1 or n % 2:
        return lax.all_gather(local, axis, axis=0, tiled=True)
    ring = snake_ring(n)
    me = lax.axis_index(axis)
    my_pos = jnp.where(me % 2 == 0, me // 2, n - (me + 1) // 2)

    def tok_at(p):
        p = p % n
        return jnp.where(p < n // 2, 2 * p, 2 * (n - 1 - p) + 1)

    cw = [(ring[i], ring[(i + 1) % n]) for i in range(n)]
    ccw = [(ring[(i + 1) % n], ring[i]) for i in range(n)]
    width = cols // (2 * pieces)
    parts = [local[:, j * width:(j + 1) * width] for j in range(2 * pieces)]
    full = jnp.zeros((n * rows, cols), local.dtype)
    for k in range(1, n):
        from_cw = tok_at(my_pos - k + n)
        from_ccw = tok_at(my_pos + k)
        for j in range(2 * pieces):
            clockwise = j % 2 == 0
            parts[j] = lax.ppermute(parts[j], axis, cw if clockwise else ccw)
            origin = from_cw if clockwise else from_ccw
            full = lax.dynamic_update_slice(full, parts[j], (origin * rows, j * width))
            if on_piece is not None:
                on_piece(origin, j, parts[j])
    full, local = lax.optimization_barrier((full, local))
    return lax.dynamic_update_slice(full, local, (me * rows, 0))


def tree_sum(v, axis):
    n = lax.axis_size(axis)
    if n & (n - 1):
        return lax.psum(v, axis)
    b = 1
    while b < n:
        v = v + lax.ppermute(v, axis, [(i, i ^ b) for i in range(n)])
        b *= 2
    return v


def packed_score(packed, count, size):
    gram = [[packed[m * count + k] for k in range(count)] for m in range(count)]
    member_obs = [packed[count * count + m] for m in range(count)]
    obs_sq = packed[count * count + count]
    diag = [gram[m][m] for m in range(count)]
    to_obs = [jnp.sqrt((diag[m] - 2.0 * member_obs[m] + obs_sq) / size + epsilon) for m in range(count)]
    pair = [[None] * count for _ in range(count)]
    pair_total = 0.0
    for m in range(count):
        for k in range(count):
            if m != k:
                pair[m][k] = jnp.sqrt((diag[m] + diag[k] - 2.0 * gram[m][k]) / size + epsilon)
                pair_total = pair_total + pair[m][k]
    energy = sum(to_obs) / count - pair_total / (2.0 * count * (count - 1))
    obs_coeff = [1.0 / (count * to_obs[m]) for m in range(count)]
    rows = []
    for m in range(count):
        row = []
        off = 0.0
        for k in range(count):
            if m != k:
                c = 1.0 / (count * (count - 1) * pair[m][k])
                off = off + c
                row.append(c)
            else:
                row.append(None)
        row[m] = obs_coeff[m] - off
        rows.append(jnp.stack(row))
    return (energy, jnp.stack(rows), -jnp.stack(obs_coeff))


def per_device(inputs, obs, weights, gains):
    sec = lax.axis_index("section")
    on_first = sec == 0
    gain = gains[0]
    tok_rows = obs.shape[0]
    width = obs.shape[1]
    size = float(tok_rows * lax.axis_size("tok") * width)

    obs_sq = jnp.einsum("rd,rd->", obs, obs, preferred_element_type=jnp.float32)

    members = inputs.shape[0]
    rows_all = inputs.reshape(members * tok_rows, width)
    n_tok = lax.axis_size("tok")
    local = weights[0]
    rows_w = local.shape[0]
    pieces = 2
    piece_w = width // (2 * pieces)
    overlap = RING_GATHER and n_tok % 2 == 0 and 2 < n_tok <= 16

    if overlap:
        acc = [None] * (2 * pieces)
        normed = []

        def on_piece(origin, j, piece):
            if not normed:
                rows_in, piece = lax.optimization_barrier((rows_all, piece))
                normed.append(norm_part(rows_in, gain))
            normed_a = normed[0][3]
            lhs = lax.dynamic_slice(normed_a, (0, origin * rows_w), (normed_a.shape[0], rows_w))
            term = jnp.dot(lhs, piece, preferred_element_type=jnp.float32)
            acc[j] = term if acc[j] is None else acc[j] + term

        weight = ring_gather(local, "tok", pieces, on_piece)
        values_a, unit_a, std_a, normed_a = normed[0]
        me = lax.axis_index("tok")
        lhs = lax.dynamic_slice(normed_a, (0, me * rows_w), (normed_a.shape[0], rows_w))
        for j in range(2 * pieces):
            acc[j] = acc[j] + jnp.dot(
                lhs, local[:, j * piece_w:(j + 1) * piece_w], preferred_element_type=jnp.float32
            )
        pre_a = jnp.concatenate(acc, axis=1)
        out_a = (values_a + gelu_value(pre_a)).astype(jnp.bfloat16)
        fa = (out_a, unit_a, std_a, pre_a)
    else:
        if RING_GATHER:
            weight = ring_gather(local, "tok")
        else:
            weight = lax.all_gather(weights, "tok", axis=1, tiled=True)[0]
        inputs, weight = lax.optimization_barrier((inputs, weight))
        rows_all = inputs.reshape(members * tok_rows, width)
        fa = section_forward(rows_all, gain, weight)
    if overlap:
        halves = []
        for m in range(members):
            rows_m = slice(m * tok_rows, (m + 1) * tok_rows)
            out_m = (values_a[rows_m] + gelu_value(pre_a[rows_m])).astype(jnp.bfloat16)
            halves.append(shifted(out_m, "section", 1))
        arrived = jnp.concatenate(halves, axis=0)
    else:
        arrived = shifted(fa[0], "section", 1)
    fb = section_forward(arrived, gain, weight)

    y = fb[0].reshape(members, tok_rows, width)
    obs_f = obs.astype(jnp.float32)
    yf = y.astype(jnp.float32)
    terms = []
    for m in range(members):
        for k in range(members):
            terms.append(jnp.sum(yf[m] * yf[k], axis=-1))
    for m in range(members):
        terms.append(jnp.sum(yf[m] * obs_f, axis=-1))
    terms = jnp.sum(jnp.stack(terms), axis=-1)
    packed = tree_sum(jnp.concatenate([terms, obs_sq.reshape(1)]), "tok")
    slope_a, slope_b = lax.optimization_barrier((gelu_slope(fa[3]), gelu_slope(fb[3])))
    member_gram = packed[: members * members].reshape(members, members)
    obs_rows = packed[members * members : members * members + members]
    obs_total = packed[members * members + members]
    energy, member_coeff, obs_coeff = score_terms(member_gram, obs_rows, obs_total, size)
    energy_arr = jnp.reshape(energy, (1,))

    def second_backward():
        cot = obs_coeff[:, None, None] * obs_f[None]
        for k in range(members):
            cot = cot + member_coeff[:, k, None, None] * y[k].astype(jnp.float32)[None]
        cot = cot.reshape(members * tok_rows, width)
        return section_backward(cot, gain, weight, fb[1], fb[2], slope_b)

    da = lax.cond(on_first, lambda: jnp.zeros((members * tok_rows, width), jnp.bfloat16), second_backward)
    back, energy_peer = shifted((da, energy_arr), "section", -1)
    energy_out = jnp.where(on_first, energy_peer, energy_arr)
    grads = lax.cond(
        on_first,
        lambda: section_backward(back.astype(jnp.float32), gain, weight, fa[1], fa[2], slope_a),
        lambda: da,
    )
    grads = grads.reshape(members, tok_rows, width)
    return (grads[None], energy_out)


def solution(mesh):
    in_specs = (
        P("groups", "tok", None),
        P(("groups", "tok"), None),
        P("section", "tok", None),
        P("section", None),
    )
    out_specs = (P("section", "groups", "tok", None), P("groups"))
    return jax.shard_map(
        per_device, mesh=mesh, in_specs=in_specs, out_specs=out_specs, check_vma=False
    )
```

```python
import math

import jax
import jax.numpy as jnp
from jax import lax
from jax.sharding import PartitionSpec as P

epsilon = 1e-05
gelu_scale = math.sqrt(2.0 / math.pi)
cubic_term = 0.044715

RING_GATHER = True


def shifted(x, axis, by):
    size = lax.axis_size(axis)
    pairs = [(i, i + by) for i in range(size) if 0 <= i + by < size]
    return lax.ppermute(x, axis, pairs)


def gelu_value(pre_act):
    inner = jnp.tanh(gelu_scale * (pre_act + cubic_term * pre_act * pre_act * pre_act))
    return 0.5 * pre_act * (1.0 + inner)


def gelu_slope(pre_act):
    inner = jnp.tanh(gelu_scale * (pre_act + cubic_term * pre_act * pre_act * pre_act))
    return 0.5 * (1.0 + inner) + 0.5 * pre_act * (1.0 - inner * inner) * gelu_scale * (
        1.0 + 3.0 * cubic_term * pre_act * pre_act
    )


def norm_part(rows_in, gain):
    values = rows_in.astype(jnp.float32)
    row_mean = jnp.mean(values, axis=-1, keepdims=True)
    centred = values - row_mean
    inv_std = lax.rsqrt(jnp.mean(centred * centred, axis=-1, keepdims=True) + epsilon)
    unit_rows = centred * inv_std
    normed = (unit_rows * gain).astype(jnp.bfloat16)
    return (values, unit_rows, inv_std, normed)


def section_forward(rows_in, gain, weight):
    values = rows_in.astype(jnp.float32)
    row_mean = jnp.mean(values, axis=-1, keepdims=True)
    centred = values - row_mean
    inv_std = lax.rsqrt(jnp.mean(centred * centred, axis=-1, keepdims=True) + epsilon)
    unit_rows = centred * inv_std
    normed = (unit_rows * gain).astype(jnp.bfloat16)
    pre_act = jnp.dot(normed, weight, preferred_element_type=jnp.float32)
    output = (values + gelu_value(pre_act)).astype(jnp.bfloat16)
    return (output, unit_rows, inv_std, pre_act)


def section_backward(grad_out, gain, weight, unit_rows, inv_std, slope, split=False):
    grad_pre = (grad_out * slope).astype(jnp.bfloat16)
    if split:
        grad_pre = lax.optimization_barrier(grad_pre)
    grad_norm = lax.dot_general(
        grad_pre, weight, (((1,), (1,)), ((), ())), preferred_element_type=jnp.float32
    )
    scaled = grad_norm * gain
    grad_in = grad_out + inv_std * (
        scaled
        - jnp.mean(scaled, axis=-1, keepdims=True)
        - unit_rows * jnp.mean(scaled * unit_rows, axis=-1, keepdims=True)
    )
    return grad_in.astype(jnp.bfloat16)


def score_terms(member_gram, member_obs, obs_sq, size):
    count = member_gram.shape[0]
    diag_vals = jnp.diagonal(member_gram)
    apart = diag_vals[:, None] + diag_vals[None, :] - 2.0 * member_gram
    same = jnp.eye(count, dtype=jnp.float32)
    others = 1.0 - same
    pair_dist = jnp.sqrt(jnp.where(same > 0.5, size, apart) / size + epsilon)
    to_obs = jnp.sqrt((diag_vals - 2.0 * member_obs + obs_sq) / size + epsilon)
    energy = jnp.mean(to_obs) - jnp.sum(others * pair_dist) / (2.0 * count * (count - 1))
    pair_coeff = others / (count * (count - 1) * pair_dist)
    obs_coeff = 1.0 / (count * to_obs)
    member_coeff = pair_coeff + same * (obs_coeff - jnp.sum(pair_coeff, axis=1))[:, None]
    return (energy, member_coeff, -obs_coeff)


def snake_ring(n):
    if n % 2:
        return list(range(n))
    return list(range(0, n, 2)) + list(range(n - 1, 0, -2))


def ring_gather(local, axis, pieces=2, on_piece=None):
    n = lax.axis_size(axis)
    rows, cols = local.shape
    if n == 1 or n % 2:
        return lax.all_gather(local, axis, axis=0, tiled=True)
    ring = snake_ring(n)
    me = lax.axis_index(axis)
    my_pos = jnp.where(me % 2 == 0, me // 2, n - (me + 1) // 2)

    def tok_at(p):
        p = p % n
        return jnp.where(p < n // 2, 2 * p, 2 * (n - 1 - p) + 1)

    cw = [(ring[i], ring[(i + 1) % n]) for i in range(n)]
    ccw = [(ring[(i + 1) % n], ring[i]) for i in range(n)]
    width = cols // (2 * pieces)
    parts = [local[:, j * width:(j + 1) * width] for j in range(2 * pieces)]
    full = jnp.zeros((n * rows, cols), local.dtype)
    for k in range(1, n):
        from_cw = tok_at(my_pos - k + n)
        from_ccw = tok_at(my_pos + k)
        for j in range(2 * pieces):
            clockwise = j % 2 == 0
            parts[j] = lax.ppermute(parts[j], axis, cw if clockwise else ccw)
            origin = from_cw if clockwise else from_ccw
            full = lax.dynamic_update_slice(full, parts[j], (origin * rows, j * width))
            if on_piece is not None:
                on_piece(origin, j, parts[j])
    full, local = lax.optimization_barrier((full, local))
    return lax.dynamic_update_slice(full, local, (me * rows, 0))


def tree_sum(v, axis):
    n = lax.axis_size(axis)
    if n & (n - 1):
        return lax.psum(v, axis)
    b = 1
    while b < n:
        v = v + lax.ppermute(v, axis, [(i, i ^ b) for i in range(n)])
        b *= 2
    return v


def packed_score(packed, count, size):
    gram = [[packed[m * count + k] for k in range(count)] for m in range(count)]
    member_obs = [packed[count * count + m] for m in range(count)]
    obs_sq = packed[count * count + count]
    diag = [gram[m][m] for m in range(count)]
    to_obs = [jnp.sqrt((diag[m] - 2.0 * member_obs[m] + obs_sq) / size + epsilon) for m in range(count)]
    pair = [[None] * count for _ in range(count)]
    pair_total = 0.0
    for m in range(count):
        for k in range(count):
            if m != k:
                pair[m][k] = jnp.sqrt((diag[m] + diag[k] - 2.0 * gram[m][k]) / size + epsilon)
                pair_total = pair_total + pair[m][k]
    energy = sum(to_obs) / count - pair_total / (2.0 * count * (count - 1))
    obs_coeff = [1.0 / (count * to_obs[m]) for m in range(count)]
    rows = []
    for m in range(count):
        row = []
        off = 0.0
        for k in range(count):
            if m != k:
                c = 1.0 / (count * (count - 1) * pair[m][k])
                off = off + c
                row.append(c)
            else:
                row.append(None)
        row[m] = obs_coeff[m] - off
        rows.append(jnp.stack(row))
    return (energy, jnp.stack(rows), -jnp.stack(obs_coeff))


def per_device(inputs, obs, weights, gains):
    sec = lax.axis_index("section")
    on_first = sec == 0
    gain = gains[0]
    tok_rows = obs.shape[0]
    width = obs.shape[1]
    size = float(tok_rows * lax.axis_size("tok") * width)

    obs_sq = jnp.einsum("rd,rd->", obs, obs, preferred_element_type=jnp.float32)

    members = inputs.shape[0]
    rows_all = inputs.reshape(members * tok_rows, width)
    n_tok = lax.axis_size("tok")
    local = weights[0]
    rows_w = local.shape[0]
    pieces = 2
    piece_w = width // (2 * pieces)
    overlap = RING_GATHER and n_tok % 2 == 0 and 2 < n_tok <= 16

    if overlap:
        acc = [None] * (2 * pieces)
        normed = []

        def on_piece(origin, j, piece):
            if not normed:
                rows_in, piece = lax.optimization_barrier((rows_all, piece))
                normed.append(norm_part(rows_in, gain))
            normed_a = normed[0][3]
            lhs = lax.dynamic_slice(normed_a, (0, origin * rows_w), (normed_a.shape[0], rows_w))
            term = jnp.dot(lhs, piece, preferred_element_type=jnp.float32)
            acc[j] = term if acc[j] is None else acc[j] + term

        weight = ring_gather(local, "tok", pieces, on_piece)
        values_a, unit_a, std_a, normed_a = normed[0]
        me = lax.axis_index("tok")
        lhs = lax.dynamic_slice(normed_a, (0, me * rows_w), (normed_a.shape[0], rows_w))
        for j in range(2 * pieces):
            acc[j] = acc[j] + jnp.dot(
                lhs, local[:, j * piece_w:(j + 1) * piece_w], preferred_element_type=jnp.float32
            )
        pre_a = jnp.concatenate(acc, axis=1)
        out_a = (values_a + gelu_value(pre_a)).astype(jnp.bfloat16)
        fa = (out_a, unit_a, std_a, pre_a)
    else:
        if RING_GATHER:
            weight = ring_gather(local, "tok")
        else:
            weight = lax.all_gather(weights, "tok", axis=1, tiled=True)[0]
        inputs, weight = lax.optimization_barrier((inputs, weight))
        rows_all = inputs.reshape(members * tok_rows, width)
        fa = section_forward(rows_all, gain, weight)
    arrived = shifted(fa[0], "section", 1)
    fb = section_forward(arrived, gain, weight)

    y = fb[0].reshape(members, tok_rows, width)
    obs_f = obs.astype(jnp.float32)
    yf = y.astype(jnp.float32)
    terms = []
    for m in range(members):
        for k in range(members):
            terms.append(jnp.sum(yf[m] * yf[k], axis=-1))
    for m in range(members):
        terms.append(jnp.sum(yf[m] * obs_f, axis=-1))
    terms = jnp.sum(jnp.stack(terms), axis=-1)
    packed = tree_sum(jnp.concatenate([terms, obs_sq.reshape(1)]), "tok")
    slope_a, slope_b = lax.optimization_barrier((gelu_slope(fa[3]), gelu_slope(fb[3])))
    member_gram = packed[: members * members].reshape(members, members)
    obs_rows = packed[members * members : members * members + members]
    obs_total = packed[members * members + members]
    energy, member_coeff, obs_coeff = score_terms(member_gram, obs_rows, obs_total, size)
    energy_arr = jnp.reshape(energy, (1,))

    def second_backward():
        cot = obs_coeff[:, None, None] * obs_f[None]
        for k in range(members):
            cot = cot + member_coeff[:, k, None, None] * y[k].astype(jnp.float32)[None]
        cot = cot.reshape(members * tok_rows, width)
        return section_backward(cot, gain, weight, fb[1], fb[2], slope_b)

    da = lax.cond(on_first, lambda: jnp.zeros((members * tok_rows, width), jnp.bfloat16), second_backward)
    back, energy_peer = shifted((da, energy_arr), "section", -1)
    energy_out = jnp.where(on_first, energy_peer, energy_arr)
    grads = lax.cond(
        on_first,
        lambda: section_backward(back.astype(jnp.float32), gain, weight, fa[1], fa[2], slope_a, True),
        lambda: da,
    )
    grads = grads.reshape(members, tok_rows, width)
    return (grads[None], energy_out)


def solution(mesh):
    in_specs = (
        P("groups", "tok", None),
        P(("groups", "tok"), None),
        P("section", "tok", None),
        P("section", None),
    )
    out_specs = (P("section", "groups", "tok", None), P("groups"))
    return jax.shard_map(
        per_device, mesh=mesh, in_specs=in_specs, out_specs=out_specs, check_vma=False
    )
```

```python
import math

import jax
import jax.numpy as jnp
from jax import lax
from jax.sharding import PartitionSpec as P

epsilon = 1e-05
gelu_scale = math.sqrt(2.0 / math.pi)
cubic_term = 0.044715

RING_GATHER = True


def shifted(x, axis, by):
    size = lax.axis_size(axis)
    pairs = [(i, i + by) for i in range(size) if 0 <= i + by < size]
    return lax.ppermute(x, axis, pairs)


def gelu_value(pre_act):
    inner = jnp.tanh(gelu_scale * (pre_act + cubic_term * pre_act * pre_act * pre_act))
    return 0.5 * pre_act * (1.0 + inner)


def gelu_slope(pre_act):
    inner = jnp.tanh(gelu_scale * (pre_act + cubic_term * pre_act * pre_act * pre_act))
    return 0.5 * (1.0 + inner) + 0.5 * pre_act * (1.0 - inner * inner) * gelu_scale * (
        1.0 + 3.0 * cubic_term * pre_act * pre_act
    )


def norm_part(rows_in, gain):
    values = rows_in.astype(jnp.float32)
    row_mean = jnp.mean(values, axis=-1, keepdims=True)
    centred = values - row_mean
    inv_std = lax.rsqrt(jnp.mean(centred * centred, axis=-1, keepdims=True) + epsilon)
    unit_rows = centred * inv_std
    normed = (unit_rows * gain).astype(jnp.bfloat16)
    return (values, unit_rows, inv_std, normed)


def section_forward(rows_in, gain, weight):
    values = rows_in.astype(jnp.float32)
    row_mean = jnp.mean(values, axis=-1, keepdims=True)
    centred = values - row_mean
    inv_std = lax.rsqrt(jnp.mean(centred * centred, axis=-1, keepdims=True) + epsilon)
    unit_rows = centred * inv_std
    normed = (unit_rows * gain).astype(jnp.bfloat16)
    pre_act = jnp.dot(normed, weight, preferred_element_type=jnp.float32)
    output = (values + gelu_value(pre_act)).astype(jnp.bfloat16)
    return (output, unit_rows, inv_std, pre_act)


def section_backward(grad_out, gain, weight, unit_rows, inv_std, slope):
    grad_pre = (grad_out * slope).astype(jnp.bfloat16)
    grad_norm = lax.dot_general(
        grad_pre, weight, (((1,), (1,)), ((), ())), preferred_element_type=jnp.float32
    )
    scaled = grad_norm * gain
    grad_in = grad_out + inv_std * (
        scaled
        - jnp.mean(scaled, axis=-1, keepdims=True)
        - unit_rows * jnp.mean(scaled * unit_rows, axis=-1, keepdims=True)
    )
    return grad_in.astype(jnp.bfloat16)


def score_terms(member_gram, member_obs, obs_sq, size):
    count = member_gram.shape[0]
    diag_vals = jnp.diagonal(member_gram)
    apart = diag_vals[:, None] + diag_vals[None, :] - 2.0 * member_gram
    same = jnp.eye(count, dtype=jnp.float32)
    others = 1.0 - same
    pair_dist = jnp.sqrt(jnp.where(same > 0.5, size, apart) / size + epsilon)
    to_obs = jnp.sqrt((diag_vals - 2.0 * member_obs + obs_sq) / size + epsilon)
    energy = jnp.mean(to_obs) - jnp.sum(others * pair_dist) / (2.0 * count * (count - 1))
    pair_coeff = others / (count * (count - 1) * pair_dist)
    obs_coeff = 1.0 / (count * to_obs)
    member_coeff = pair_coeff + same * (obs_coeff - jnp.sum(pair_coeff, axis=1))[:, None]
    return (energy, member_coeff, -obs_coeff)


def snake_ring(n):
    if n % 2:
        return list(range(n))
    return list(range(0, n, 2)) + list(range(n - 1, 0, -2))


def ring_gather(local, axis, pieces=2, on_piece=None):
    n = lax.axis_size(axis)
    rows, cols = local.shape
    if n == 1 or n % 2:
        return lax.all_gather(local, axis, axis=0, tiled=True)
    ring = snake_ring(n)
    me = lax.axis_index(axis)
    my_pos = jnp.where(me % 2 == 0, me // 2, n - (me + 1) // 2)

    def tok_at(p):
        p = p % n
        return jnp.where(p < n // 2, 2 * p, 2 * (n - 1 - p) + 1)

    cw = [(ring[i], ring[(i + 1) % n]) for i in range(n)]
    ccw = [(ring[(i + 1) % n], ring[i]) for i in range(n)]
    width = cols // (2 * pieces)
    parts = [local[:, j * width:(j + 1) * width] for j in range(2 * pieces)]
    full = jnp.zeros((n * rows, cols), local.dtype)
    for k in range(1, n):
        from_cw = tok_at(my_pos - k + n)
        from_ccw = tok_at(my_pos + k)
        for j in range(2 * pieces):
            clockwise = j % 2 == 0
            parts[j] = lax.ppermute(parts[j], axis, cw if clockwise else ccw)
            origin = from_cw if clockwise else from_ccw
            full = lax.dynamic_update_slice(full, parts[j], (origin * rows, j * width))
            if on_piece is not None:
                on_piece(origin, j, parts[j])
    full, local = lax.optimization_barrier((full, local))
    return lax.dynamic_update_slice(full, local, (me * rows, 0))


def tree_sum(v, axis):
    n = lax.axis_size(axis)
    if n & (n - 1):
        return lax.psum(v, axis)
    b = 1
    while b < n:
        v = v + lax.ppermute(v, axis, [(i, i ^ b) for i in range(n)])
        b *= 2
    return v


def packed_score(packed, count, size):
    gram = [[packed[m * count + k] for k in range(count)] for m in range(count)]
    member_obs = [packed[count * count + m] for m in range(count)]
    obs_sq = packed[count * count + count]
    diag = [gram[m][m] for m in range(count)]
    to_obs = [jnp.sqrt((diag[m] - 2.0 * member_obs[m] + obs_sq) / size + epsilon) for m in range(count)]
    pair = [[None] * count for _ in range(count)]
    pair_total = 0.0
    for m in range(count):
        for k in range(count):
            if m != k:
                pair[m][k] = jnp.sqrt((diag[m] + diag[k] - 2.0 * gram[m][k]) / size + epsilon)
                pair_total = pair_total + pair[m][k]
    energy = sum(to_obs) / count - pair_total / (2.0 * count * (count - 1))
    obs_coeff = [1.0 / (count * to_obs[m]) for m in range(count)]
    rows = []
    for m in range(count):
        row = []
        off = 0.0
        for k in range(count):
            if m != k:
                c = 1.0 / (count * (count - 1) * pair[m][k])
                off = off + c
                row.append(c)
            else:
                row.append(None)
        row[m] = obs_coeff[m] - off
        rows.append(jnp.stack(row))
    return (energy, jnp.stack(rows), -jnp.stack(obs_coeff))


def per_device(inputs, obs, weights, gains):
    sec = lax.axis_index("section")
    on_first = sec == 0
    gain = gains[0]
    tok_rows = obs.shape[0]
    width = obs.shape[1]
    size = float(tok_rows * lax.axis_size("tok") * width)

    obs_sq = jnp.einsum("rd,rd->", obs, obs, preferred_element_type=jnp.float32)

    members = inputs.shape[0]
    rows_all = inputs.reshape(members * tok_rows, width)
    n_tok = lax.axis_size("tok")
    local = weights[0]
    rows_w = local.shape[0]
    pieces = 2
    piece_w = width // (2 * pieces)
    overlap = RING_GATHER and n_tok % 2 == 0 and 2 < n_tok <= 16

    if overlap:
        acc = [None] * (2 * pieces)
        normed = []
        calls = []

        def on_piece(origin, j, piece):
            if not normed:
                rows_in, piece = lax.optimization_barrier((rows_all, piece))
                normed.append(norm_part(rows_in, gain))
            normed_a = normed[0][3]
            lhs = lax.dynamic_slice(normed_a, (0, origin * rows_w), (normed_a.shape[0], rows_w))
            term = jnp.dot(lhs, piece, preferred_element_type=jnp.float32)
            acc[j] = term if acc[j] is None else acc[j] + term
            calls.append(j)
            if len(calls) == 4 * pieces + 1:
                me = lax.axis_index("tok")
                own, _ = lax.optimization_barrier((
                    lax.dynamic_slice(normed_a, (0, me * rows_w), (normed_a.shape[0], rows_w)),
                    piece,
                ))
                for i in range(2 * pieces):
                    acc[i] = acc[i] + jnp.dot(
                        own, local[:, i * piece_w:(i + 1) * piece_w],
                        preferred_element_type=jnp.float32,
                    )

        weight = ring_gather(local, "tok", pieces, on_piece)
        values_a, unit_a, std_a, normed_a = normed[0]
        pre_a = jnp.concatenate(acc, axis=1)
        out_a = (values_a + gelu_value(pre_a)).astype(jnp.bfloat16)
        fa = (out_a, unit_a, std_a, pre_a)
    else:
        if RING_GATHER:
            weight = ring_gather(local, "tok")
        else:
            weight = lax.all_gather(weights, "tok", axis=1, tiled=True)[0]
        inputs, weight = lax.optimization_barrier((inputs, weight))
        rows_all = inputs.reshape(members * tok_rows, width)
        fa = section_forward(rows_all, gain, weight)
    arrived = shifted(fa[0], "section", 1)
    fb = section_forward(arrived, gain, weight)

    y = fb[0].reshape(members, tok_rows, width)
    obs_f = obs.astype(jnp.float32)
    yf = y.astype(jnp.float32)
    terms = []
    for m in range(members):
        for k in range(members):
            terms.append(jnp.sum(yf[m] * yf[k], axis=-1))
    for m in range(members):
        terms.append(jnp.sum(yf[m] * obs_f, axis=-1))
    terms = jnp.sum(jnp.stack(terms), axis=-1)
    packed = tree_sum(jnp.concatenate([terms, obs_sq.reshape(1)]), "tok")
    slope_a, slope_b = lax.optimization_barrier((gelu_slope(fa[3]), gelu_slope(fb[3])))
    member_gram = packed[: members * members].reshape(members, members)
    obs_rows = packed[members * members : members * members + members]
    obs_total = packed[members * members + members]
    energy, member_coeff, obs_coeff = score_terms(member_gram, obs_rows, obs_total, size)
    energy_arr = jnp.reshape(energy, (1,))

    def second_backward():
        cot = obs_coeff[:, None, None] * obs_f[None]
        for k in range(members):
            cot = cot + member_coeff[:, k, None, None] * y[k].astype(jnp.float32)[None]
        cot = cot.reshape(members * tok_rows, width)
        return section_backward(cot, gain, weight, fb[1], fb[2], slope_b)

    da = lax.cond(on_first, lambda: jnp.zeros((members * tok_rows, width), jnp.bfloat16), second_backward)
    back, energy_peer = shifted((da, energy_arr), "section", -1)
    energy_out = jnp.where(on_first, energy_peer, energy_arr)
    grads = lax.cond(
        on_first,
        lambda: section_backward(back.astype(jnp.float32), gain, weight, fa[1], fa[2], slope_a),
        lambda: da,
    )
    grads = grads.reshape(members, tok_rows, width)
    return (grads[None], energy_out)


def solution(mesh):
    in_specs = (
        P("groups", "tok", None),
        P(("groups", "tok"), None),
        P("section", "tok", None),
        P("section", None),
    )
    out_specs = (P("section", "groups", "tok", None), P("groups"))
    return jax.shard_map(
        per_device, mesh=mesh, in_specs=in_specs, out_specs=out_specs, check_vma=False
    )
```
